256 devices in a mesh: nodes: 64 (over z, y, core), mp: 4 (over x).
Axes of the slice: x: 4, y: 4, z: 8, core: 2. Of those that a mesh axis runs over, the one named last changes fastest.
Arguments:
- event_feats: bfloat16 [65536, 512], P('nodes'), may hold values from -6 to 6
- event_owner: int32 [65536, 1], P('nodes'), may hold values from 0 to 63; in each aligned block of 1024 rows (0 to 1023, 1024 to 2047, ...) at most 32 rows name the same one
- event_slot: int32 [65536], P('nodes'), may hold values from 0 to 255
- memory: bfloat16 [16384, 1024], P('nodes'), may hold values from -6 to 6
- w_msg_event: bfloat16 [512, 2048], P(None, 'mp'), may hold values from -0.25 to 0.25
- w_msg_state: bfloat16 [1024, 2048], P(None, 'mp'), may hold values from -0.1875 to 0.1875
- b_msg: float32 [2048], P('mp'), may hold values from -3 to 3
- w_msg_out: bfloat16 [2048, 1024], P('mp'), may hold values from -0.125 to 0.125
- b_out: float32 [1024], replicated, may hold values from -3 to 3
- w_input: bfloat16 [3, 1024, 1024], P(None, None, 'mp'), may hold values from -0.1875 to 0.1875
- w_hidden: bfloat16 [3, 1024, 1024], P(None, None, 'mp'), may hold values from -0.1875 to 0.1875
- b_input: float32 [3, 1024], P(None, 'mp'), may hold values from -3 to 3
- b_hidden: float32 [3, 1024], P(None, 'mp'), may hold values from -3 to 3
- state_slots: int32 [4096, 32], P('nodes'), may hold values from 0 to 255
- neighbours: int32 [16384, 10], P('nodes'), may hold values from 0 to 2047
- query_slots: int32 [16384], P('nodes'), may hold values from 0 to 255
- w_neigh: bfloat16 [1024, 1024], P('mp'), may hold values from -0.1875 to 0.1875
- w_self: bfloat16 [1024, 1024], P('mp'), may hold values from -0.1875 to 0.1875
- b_embed: float32 [1024], replicated, may hold values from -3 to 3
Outputs:
- new_memory: bfloat16 [16384, 1024], P('nodes', 'mp')
- embedding: bfloat16 [16384, 1024], P(('nodes', 'mp'))
The draws below stay inside these ranges and needn't reach their ends.
Inputs may be any that keep to these rules, and one draw needn't show every extreme that they name: `event_owner`: among the 1024 events of one block of events, at most 32 name the same owner, and in every draw some owner is named exactly 32 times by some block.
All inputs are finite; a program needn't handle non-finite values.
Results may differ from the reference program's by a relative error of at most 0.014.
Values may be sent and summed in bfloat16 or wider, within the bound.
No kernel may reach another device: no remote copies, remote signals or barrier semaphores. Data moves between devices by JAX's collectives and lax.ppermute only.
A program may use at most 64 MiB of HBM per device.

```python
import math
import jax
import jax.numpy as jnp
import numpy as np
from jax import lax

DM = 1024
FEAT = 512
MH = 2048
NEIGH = 10
STATE_CAP = 32
E_DEV = 1024
M_DEV = 256
Q_DEV = 256
OWNERS = 64
CAP = 32
EVENTS = 65536
NODES = 16384
QUERIES = 16384
N_NODES = 64


def place_ends(entries, key, least, top_value):
    longest = entries.shape.index(max(entries.shape))
    spots = []
    for shift in (0, 1):
        where = [jax.random.randint(jax.random.fold_in(key, axis), (), 0, length) for axis, length in enumerate(entries.shape)]
        where[longest] = (where[longest] + shift) % entries.shape[longest]
        spots.append(tuple(where))
    return entries.at[spots[0]].set(least).at[spots[1]].set(top_value)


def levels(rng, dims, cuts, least, top_value):
    gain = 1.0
    for axis_at, shards_of in cuts:
        draws = jax.random.uniform(jax.random.fold_in(jax.random.fold_in(rng, 6), axis_at), (shards_of,), jnp.float32, least / len(cuts), top_value / len(cuts))
        gain = gain * jnp.repeat(jnp.exp(draws), dims[axis_at] // shards_of).reshape((-1,) + (1,) * (len(dims) - 1 - axis_at))
    return gain


def routed_block(stream_key, own, number, rows, count, top, reach, slope):
    sequence = jax.random.permutation(stream_key, count)
    packed, common = shares(count, rows * top, reach, slope, True), shares(count, rows * top, reach, slope, False)
    places = jnp.arange(count)

    def named(tallies, offset_by):
        used = int((tallies > 0).sum())
        fixed = max(1, used // 4)
        passed = fixed + (places - fixed + offset_by * (used - fixed)) % max(1, count - fixed)
        return jnp.zeros((count,), jnp.int32).at[sequence[jnp.where(places < fixed, places, passed)]].set(jnp.asarray(tallies, jnp.int32))

    tallies = jnp.where(number % 4 == 0, named(packed, number // 4), named(common, number - number // 4 - 1))
    mixed = jax.random.permutation(jax.random.fold_in(own, 3), count)
    donor, receiver = mixed[0:count // 2 * 2:2], mixed[1:count // 2 * 2:2]
    room = jnp.minimum(tallies[donor] - 1, reach - tallies[receiver]) // 2
    room = jnp.where((donor == sequence[0]) | (receiver == sequence[0]) | (tallies[receiver] == 0), 0, jnp.maximum(room, 0))
    passed = jax.random.randint(jax.random.fold_in(own, 4), (count // 2,), 0, 1 << 20) % (room + 1)
    tallies = tallies.at[donor].add(-passed).at[receiver].add(passed)
    members = jnp.searchsorted(jnp.cumsum(tallies), jnp.arange(rows * top), side="right").astype(jnp.int32)
    grid = members.reshape(top, rows).T
    grid = grid[jax.random.permutation(jax.random.fold_in(own, 1), rows)]
    offset_by = jax.random.randint(jax.random.fold_in(own, 2), (rows, 1), 0, top)
    return jnp.take_along_axis(grid, (jnp.arange(top)[None, :] + offset_by) % top, axis=1)


def shares(number_of, total, most, slope, full):
    weights = [(1 << 20) // math.isqrt(standing ** slope) + 1 for standing in range(1, number_of + 1)]
    largest = most if full else min(most, max(-(-total // number_of), total * weights[0] // sum(weights)))
    least = 1 if total - largest >= number_of - 1 else 0
    holding, spare = [largest] + [least] * (number_of - 1), total - largest - least * (number_of - 1)
    while spare > 0:
        candidates = [i for i in range(1, number_of) if holding[i] < largest] or [i for i in range(1, number_of) if holding[i] < most]
        mass, remaining = sum([weights[i] for i in candidates]), spare
        for i in candidates:
            addition = min(most - holding[i], max(1, remaining * weights[i] // mass), spare)
            holding[i] = holding[i] + addition
            spare = spare - addition
    return np.array(holding)


def centred(stream_key, extent, scale, limit, shards=(), held_as=jnp.bfloat16):
    level = levels(stream_key, extent, shards, -0.22, 0.18) if shards else 1.0
    drawn = jax.random.normal(stream_key, extent, jnp.float32) * scale * level
    return jnp.minimum(jnp.maximum(drawn, -limit), limit).astype(held_as)


def setup_inputs(seed: int = 0) -> dict:
    seeds = jax.random.split(jax.random.key(seed), 20)
    event_feats = centred(seeds[0], (EVENTS, FEAT), 1.0, 6.0, ((0, 64),))
    event_owner_keys = jax.random.split(jax.random.fold_in(seeds[1], 1), EVENTS // E_DEV)
    event_owner_turns = jax.random.permutation(jax.random.fold_in(seeds[1], 3), EVENTS // E_DEV)
    event_owner = jax.vmap(lambda own, number: routed_block(jax.random.fold_in(seeds[1], 2), own, number, E_DEV, OWNERS, 1, CAP, 2))(event_owner_keys, event_owner_turns).reshape((EVENTS, 1))
    event_slot = place_ends(jax.random.randint(seeds[2], (EVENTS,), 0, M_DEV), jax.random.fold_in(seeds[2], 1), 0, M_DEV - 1).astype(jnp.int32)
    memory = centred(seeds[3], (NODES, DM), 1.0, 6.0, ((0, 64),))
    w_msg_event = centred(seeds[4], (FEAT, MH), FEAT ** -0.5, 0.25, ((1, 4),))
    w_msg_state = centred(seeds[5], (DM, MH), DM ** -0.5, 0.1875, ((1, 4),))
    b_msg = centred(seeds[6], (MH,), 0.5, 3.0, ((0, 4),), jnp.float32)
    w_msg_out = centred(seeds[7], (MH, DM), MH ** -0.5, 0.125, ((0, 4),))
    b_out = centred(seeds[8], (DM,), 0.5, 3.0, (), jnp.float32)
    w_input = centred(seeds[9], (3, DM, DM), DM ** -0.5, 0.1875, ((2, 4),))
    w_hidden = centred(seeds[10], (3, DM, DM), DM ** -0.5, 0.1875, ((2, 4),))
    b_input = centred(seeds[11], (3, DM), 0.5, 3.0, ((1, 4),), jnp.float32)
    b_hidden = centred(seeds[12], (3, DM), 0.5, 3.0, ((1, 4),), jnp.float32)
    state_slots = place_ends(jax.random.randint(seeds[13], (OWNERS * OWNERS, STATE_CAP), 0, M_DEV), jax.random.fold_in(seeds[13], 1), 0, M_DEV - 1).astype(jnp.int32)
    neighbours = place_ends(jax.random.randint(seeds[14], (QUERIES, NEIGH), 0, OWNERS * STATE_CAP), jax.random.fold_in(seeds[14], 1), 0, (OWNERS * STATE_CAP) - 1).astype(jnp.int32)
    query_slots = place_ends(jax.random.randint(seeds[15], (QUERIES,), 0, M_DEV), jax.random.fold_in(seeds[15], 1), 0, M_DEV - 1).astype(jnp.int32)
    w_neigh = centred(seeds[16], (DM, DM), DM ** -0.5, 0.1875, ((0, 4),))
    w_self = centred(seeds[17], (DM, DM), DM ** -0.5, 0.1875, ((0, 4),))
    b_embed = centred(seeds[18], (DM,), 0.5, 3.0, (), jnp.float32)
    return {"event_feats": event_feats, "event_owner": event_owner, "event_slot": event_slot, "memory": memory, "w_msg_event": w_msg_event, "w_msg_state": w_msg_state, "b_msg": b_msg, "w_msg_out": w_msg_out, "b_out": b_out, "w_input": w_input, "w_hidden": w_hidden, "b_input": b_input, "b_hidden": b_hidden, "state_slots": state_slots, "neighbours": neighbours, "query_slots": query_slots, "w_neigh": w_neigh, "w_self": w_self, "b_embed": b_embed}


def reference(event_feats, event_owner, event_slot, memory, w_msg_event, w_msg_state, b_msg, w_msg_out, b_out, w_input, w_hidden, b_input, b_hidden, state_slots, neighbours, query_slots, w_neigh, w_self, b_embed):
    dest = (event_owner[:, 0] * M_DEV + event_slot).astype(jnp.int32)
    state_proj = jnp.dot(memory, w_msg_state, preferred_element_type=jnp.float32)
    feats_blocks = event_feats.reshape(N_NODES, E_DEV, FEAT)
    dest_blocks = dest.reshape(N_NODES, E_DEV)

    def accumulate(carry, item):
        hidden_sum, counts = carry
        feats, targets = item
        pre = jnp.dot(feats, w_msg_event, preferred_element_type=jnp.float32) + state_proj[targets] + b_msg
        hidden_msg = jax.nn.relu(pre).astype(jnp.bfloat16)
        hidden_sum = hidden_sum.at[targets].add(hidden_msg.astype(jnp.float32))
        counts = counts.at[targets].add(jnp.ones((E_DEV,), jnp.float32))
        return (hidden_sum, counts), None

    start = (jnp.zeros((NODES, MH), jnp.float32), jnp.zeros((NODES,), jnp.float32))
    (hidden_sum, counts), unused = lax.scan(accumulate, start, (feats_blocks, dest_blocks))
    msg_total = jnp.dot(hidden_sum, w_msg_out.astype(jnp.float32), precision=lax.Precision.HIGHEST)
    aggregate = (msg_total / jnp.maximum(counts, 1.0)[:, None] + b_out).astype(jnp.bfloat16)
    gates_in = [jnp.dot(aggregate, w_input[g], preferred_element_type=jnp.float32) + b_input[g] for g in range(3)]
    gates_st = [jnp.dot(memory, w_hidden[g], preferred_element_type=jnp.float32) + b_hidden[g] for g in range(3)]
    reset_gate = jax.nn.sigmoid(gates_in[0] + gates_st[0])
    update_gate = jax.nn.sigmoid(gates_in[1] + gates_st[1])
    candidate = jnp.tanh(gates_in[2] + reset_gate * gates_st[2])
    old_state = memory.astype(jnp.float32)
    updated = (1.0 - update_gate) * candidate + update_gate * old_state
    new_memory = jnp.where((counts > 0.0)[:, None], updated, old_state).astype(jnp.bfloat16)

    block_of = (jnp.arange(QUERIES, dtype=jnp.int32) // Q_DEV).astype(jnp.int32)
    owner_of = (neighbours // STATE_CAP).astype(jnp.int32)
    place_of = (neighbours % STATE_CAP).astype(jnp.int32)
    node_of = owner_of * M_DEV + state_slots[owner_of * OWNERS + block_of[:, None], place_of]
    total = jnp.zeros((QUERIES, DM), jnp.float32)
    for k in range(NEIGH):
        total = total + new_memory[node_of[:, k]].astype(jnp.float32)
    neigh_mean = (total / NEIGH).astype(jnp.bfloat16)
    self_state = new_memory[block_of * M_DEV + query_slots]
    summed = jnp.dot(neigh_mean, w_neigh, preferred_element_type=jnp.float32) + jnp.dot(self_state, w_self, preferred_element_type=jnp.float32)
    embedding = jax.nn.relu(summed + b_embed).astype(jnp.bfloat16)
    return new_memory, embedding
```

```python
import jax
import jax.numpy as jnp
from jax import lax
from jax.sharding import PartitionSpec as P

F32 = jnp.float32
BF16 = jnp.bfloat16


def one_hot(index, size, dtype=BF16):
    return (index[:, None] == lax.broadcasted_iota(jnp.int32, (1, size), 1)).astype(dtype)


def one_hot_t(index, size, dtype=BF16):
    return (lax.broadcasted_iota(jnp.int32, (size, 1), 0) == index[None, :]).astype(dtype)


def split_dot(x32, w):
    hi = x32.astype(BF16)
    lo = (x32 - hi.astype(F32)).astype(BF16)
    return jnp.dot(hi, w, preferred_element_type=F32) + jnp.dot(lo, w, preferred_element_type=F32)


def per_device(
    event_feats,
    event_owner,
    event_slot,
    memory,
    w_msg_event,
    w_msg_state,
    b_msg,
    w_msg_out,
    b_out,
    w_input,
    w_hidden,
    b_input,
    b_hidden,
    state_slots,
    neighbours,
    query_slots,
    w_neigh,
    w_self,
    b_embed,
):
    owner_count = lax.axis_size("nodes")
    share_count = lax.axis_size("mp")
    mp_index = lax.axis_index("mp")
    event_rows = event_feats.shape[0]
    mem_rows = memory.shape[0]
    mem_width = memory.shape[1]
    col_share = mem_width // share_count
    capacity = 2 * event_rows // owner_count
    send_rows = owner_count * capacity

    owner = event_owner[:, 0]
    match = owner[:, None] == lax.broadcasted_iota(jnp.int32, (1, owner_count), 1)
    earlier = (
        lax.broadcasted_iota(jnp.int32, (event_rows, event_rows), 1)
        < lax.broadcasted_iota(jnp.int32, (event_rows, event_rows), 0)
    ).astype(BF16)
    before = jnp.dot(earlier, match.astype(BF16), preferred_element_type=F32)
    place = jnp.sum(jnp.where(match, before, 0.0), axis=1).astype(jnp.int32)
    target = owner * capacity + place

    route = one_hot_t(target, send_rows)
    feat_buffer = jnp.dot(route, event_feats, preferred_element_type=F32).astype(BF16)
    slot_col = jnp.broadcast_to((event_slot + 1).astype(BF16)[:, None], (event_rows, 128))
    id_buffer = (
        jnp.dot(route, slot_col, preferred_element_type=F32)[:, 0].astype(jnp.int32) - 1
    )
    feat_buffer = feat_buffer.reshape(owner_count, capacity, event_feats.shape[1])
    id_buffer = id_buffer.reshape(owner_count, capacity)
    arrived = lax.all_to_all(feat_buffer, "nodes", split_axis=0, concat_axis=0, tiled=True)
    arrived_ids = lax.all_to_all(id_buffer, "nodes", split_axis=0, concat_axis=0, tiled=True)
    arrived = arrived.reshape(send_rows, event_feats.shape[1])
    arrived_ids = arrived_ids.reshape(send_rows)

    seg = one_hot_t(arrived_ids, mem_rows)
    seg_t = one_hot(arrived_ids, mem_rows)
    counts = jnp.sum(seg.astype(F32), axis=1)

    state_proj = jnp.dot(memory, w_msg_state, preferred_element_type=F32)
    sp_hi = state_proj.astype(BF16)
    sp_lo = (state_proj - sp_hi.astype(F32)).astype(BF16)
    gathered = jnp.dot(seg_t, sp_hi, preferred_element_type=F32) + jnp.dot(
        seg_t, sp_lo, preferred_element_type=F32
    )
    pre = jnp.dot(arrived, w_msg_event, preferred_element_type=F32) + gathered + b_msg
    hidden_msg = jax.nn.relu(pre).astype(BF16)
    hidden_sum = jnp.dot(seg, hidden_msg, preferred_element_type=F32)
    partial_total = split_dot(hidden_sum, w_msg_out)

    divisor = jnp.maximum(counts, 1.0)[:, None]
    msg_total = lax.psum(partial_total.astype(BF16), "mp").astype(F32)
    aggregate = (msg_total / divisor + b_out).astype(BF16)
    gates_in = (
        jnp.einsum("nd,gdc->gnc", aggregate, w_input, preferred_element_type=F32)
        + b_input[:, None, :]
    )
    gates_st = (
        jnp.einsum("nd,gdc->gnc", memory, w_hidden, preferred_element_type=F32)
        + b_hidden[:, None, :]
    )
    reset_gate = jax.nn.sigmoid(gates_in[0] + gates_st[0])
    update_gate = jax.nn.sigmoid(gates_in[1] + gates_st[1])
    candidate = jnp.tanh(gates_in[2] + reset_gate * gates_st[2])
    old_state = lax.dynamic_slice_in_dim(memory, mp_index * col_share, col_share, 1).astype(F32)
    updated = (1.0 - update_gate) * candidate + update_gate * old_state
    new_memory = jnp.where((counts > 0.0)[:, None], updated, old_state).astype(BF16)

    pick = one_hot(state_slots.reshape(-1), mem_rows)
    outgoing = jnp.dot(pick, new_memory, preferred_element_type=F32).astype(BF16)
    outgoing = outgoing.reshape(state_slots.shape[0], state_slots.shape[1], col_share)
    relayed = lax.all_to_all(outgoing, "nodes", split_axis=0, concat_axis=0, tiled=True)
    relayed = relayed.reshape(relayed.shape[0] * relayed.shape[1], col_share)
    recv_rows = relayed.shape[0]
    neigh_count = one_hot(neighbours[:, 0], recv_rows, F32)
    for k in range(1, neighbours.shape[1]):
        neigh_count = neigh_count + one_hot(neighbours[:, k], recv_rows, F32)
    neigh_total = jnp.dot(neigh_count.astype(BF16), relayed, preferred_element_type=F32)
    neigh_mean = (neigh_total / neighbours.shape[1]).astype(BF16)
    self_state = jnp.dot(
        one_hot(query_slots, mem_rows), new_memory, preferred_element_type=F32
    ).astype(BF16)
    summed = lax.psum_scatter(
        (
            jnp.dot(neigh_mean, w_neigh, preferred_element_type=F32)
            + jnp.dot(self_state, w_self, preferred_element_type=F32)
        ).astype(BF16),
        "mp",
        scatter_dimension=0,
        tiled=True,
    ).astype(F32)
    embedding = jax.nn.relu(summed + b_embed).astype(BF16)
    return (new_memory, embedding)


def solution(mesh):
    in_specs = (
        P("nodes", None),
        P("nodes", None),
        P("nodes"),
        P("nodes", None),
        P(None, "mp"),
        P(None, "mp"),
        P("mp"),
        P("mp", None),
        P(),
        P(None, None, "mp"),
        P(None, None, "mp"),
        P(None, "mp"),
        P(None, "mp"),
        P("nodes", None),
        P("nodes", None),
        P("nodes"),
        P("mp", None),
        P("mp", None),
        P(),
    )
    out_specs = (P("nodes", "mp"), P(("nodes", "mp"), None))
    return jax.shard_map(
        per_device, mesh=mesh, in_specs=in_specs, out_specs=out_specs, check_vma=False
    )
```

```python
import jax
import jax.numpy as jnp
from jax import lax
from jax.sharding import PartitionSpec as P

F32 = jnp.float32
BF16 = jnp.bfloat16


def one_hot(index, size, dtype=BF16):
    return (index[:, None] == lax.broadcasted_iota(jnp.int32, (1, size), 1)).astype(dtype)


def one_hot_t(index, size, dtype=BF16):
    return (lax.broadcasted_iota(jnp.int32, (size, 1), 0) == index[None, :]).astype(dtype)


def split_dot(x32, w):
    hi = x32.astype(BF16)
    lo = (x32 - hi.astype(F32)).astype(BF16)
    return jnp.dot(hi, w, preferred_element_type=F32) + jnp.dot(lo, w, preferred_element_type=F32)


def mp_reduce_scatter(x, axis, n, me):
    rows = x.shape[0] // n
    chunks = x.reshape(n, rows, x.shape[1])
    doubled = jnp.concatenate([chunks, chunks], axis=0)
    ahead = lax.dynamic_slice_in_dim(doubled, me, n, 0)
    total = ahead[0].astype(F32)
    for t in range(1, n):
        got = lax.ppermute(ahead[t], axis, [(i, (i + t) % n) for i in range(n)])
        total = total + got.astype(F32)
    return total


def mp_all_gather(piece, axis, n, me):
    rel = [piece]
    for t in range(1, n):
        rel.append(lax.ppermute(piece, axis, [(i, (i - t) % n) for i in range(n)]))
    rel = jnp.stack(rel + rel, axis=0)
    full = lax.dynamic_slice_in_dim(rel, (n - me) % n, n, 0)
    return full.reshape(n * piece.shape[0], piece.shape[1])


def per_device(
    event_feats,
    event_owner,
    event_slot,
    memory,
    w_msg_event,
    w_msg_state,
    b_msg,
    w_msg_out,
    b_out,
    w_input,
    w_hidden,
    b_input,
    b_hidden,
    state_slots,
    neighbours,
    query_slots,
    w_neigh,
    w_self,
    b_embed,
):
    owner_count = lax.axis_size("nodes")
    share_count = lax.axis_size("mp")
    mp_index = lax.axis_index("mp")
    event_rows = event_feats.shape[0]
    mem_rows = memory.shape[0]
    mem_width = memory.shape[1]
    col_share = mem_width // share_count
    capacity = 2 * event_rows // owner_count
    send_rows = owner_count * capacity

    owner = event_owner[:, 0]
    match = owner[:, None] == lax.broadcasted_iota(jnp.int32, (1, owner_count), 1)
    earlier = (
        lax.broadcasted_iota(jnp.int32, (event_rows, event_rows), 1)
        < lax.broadcasted_iota(jnp.int32, (event_rows, event_rows), 0)
    ).astype(BF16)
    before = jnp.dot(earlier, match.astype(BF16), preferred_element_type=F32)
    place = jnp.sum(jnp.where(match, before, 0.0), axis=1).astype(jnp.int32)
    target = owner * capacity + place

    route = one_hot_t(target, send_rows)
    feat_buffer = jnp.dot(route, event_feats, preferred_element_type=F32).astype(BF16)
    slot_col = jnp.broadcast_to((event_slot + 1).astype(BF16)[:, None], (event_rows, 128))
    id_buffer = (
        jnp.dot(route, slot_col, preferred_element_type=F32)[:, 0].astype(jnp.int32) - 1
    )
    feat_buffer = feat_buffer.reshape(owner_count, capacity, event_feats.shape[1])
    id_buffer = id_buffer.reshape(owner_count, capacity)
    arrived = lax.all_to_all(feat_buffer, "nodes", split_axis=0, concat_axis=0, tiled=True)
    arrived_ids = lax.all_to_all(id_buffer, "nodes", split_axis=0, concat_axis=0, tiled=True)
    arrived = arrived.reshape(send_rows, event_feats.shape[1])
    arrived_ids = arrived_ids.reshape(send_rows)

    seg = one_hot_t(arrived_ids, mem_rows)
    seg_t = one_hot(arrived_ids, mem_rows)
    counts = jnp.sum(seg.astype(F32), axis=1)

    state_proj = jnp.dot(memory, w_msg_state, preferred_element_type=F32)
    sp_hi = state_proj.astype(BF16)
    sp_lo = (state_proj - sp_hi.astype(F32)).astype(BF16)
    gathered = jnp.dot(seg_t, sp_hi, preferred_element_type=F32) + jnp.dot(
        seg_t, sp_lo, preferred_element_type=F32
    )
    pre = jnp.dot(arrived, w_msg_event, preferred_element_type=F32) + gathered + b_msg
    hidden_msg = jax.nn.relu(pre).astype(BF16)
    hidden_sum = jnp.dot(seg, hidden_msg, preferred_element_type=F32)
    partial_total = split_dot(hidden_sum, w_msg_out)

    divisor = jnp.maximum(counts, 1.0)[:, None]
    reduced = mp_reduce_scatter(partial_total.astype(BF16), "mp", share_count, mp_index)
    msg_total = mp_all_gather(reduced.astype(BF16), "mp", share_count, mp_index).astype(F32)
    aggregate = (msg_total / divisor + b_out).astype(BF16)
    gates_in = (
        jnp.einsum("nd,gdc->gnc", aggregate, w_input, preferred_element_type=F32)
        + b_input[:, None, :]
    )
    gates_st = (
        jnp.einsum("nd,gdc->gnc", memory, w_hidden, preferred_element_type=F32)
        + b_hidden[:, None, :]
    )
    reset_gate = jax.nn.sigmoid(gates_in[0] + gates_st[0])
    update_gate = jax.nn.sigmoid(gates_in[1] + gates_st[1])
    candidate = jnp.tanh(gates_in[2] + reset_gate * gates_st[2])
    old_state = lax.dynamic_slice_in_dim(memory, mp_index * col_share, col_share, 1).astype(F32)
    updated = (1.0 - update_gate) * candidate + update_gate * old_state
    new_memory = jnp.where((counts > 0.0)[:, None], updated, old_state).astype(BF16)

    pick = one_hot(state_slots.reshape(-1), mem_rows)
    outgoing = jnp.dot(pick, new_memory, preferred_element_type=F32).astype(BF16)
    outgoing = outgoing.reshape(state_slots.shape[0], state_slots.shape[1], col_share)
    relayed = lax.all_to_all(outgoing, "nodes", split_axis=0, concat_axis=0, tiled=True)
    relayed = relayed.reshape(relayed.shape[0] * relayed.shape[1], col_share)
    recv_rows = relayed.shape[0]
    neigh_count = one_hot(neighbours[:, 0], recv_rows, F32)
    for k in range(1, neighbours.shape[1]):
        neigh_count = neigh_count + one_hot(neighbours[:, k], recv_rows, F32)
    neigh_total = jnp.dot(neigh_count.astype(BF16), relayed, preferred_element_type=F32)
    neigh_mean = (neigh_total / neighbours.shape[1]).astype(BF16)
    self_state = jnp.dot(
        one_hot(query_slots, mem_rows), new_memory, preferred_element_type=F32
    ).astype(BF16)
    summed = mp_reduce_scatter(
        (
            jnp.dot(neigh_mean, w_neigh, preferred_element_type=F32)
            + jnp.dot(self_state, w_self, preferred_element_type=F32)
        ).astype(BF16),
        "mp",
        share_count,
        mp_index,
    )
    embedding = jax.nn.relu(summed + b_embed).astype(BF16)
    return (new_memory, embedding)


def solution(mesh):
    in_specs = (
        P("nodes", None),
        P("nodes", None),
        P("nodes"),
        P("nodes", None),
        P(None, "mp"),
        P(None, "mp"),
        P("mp"),
        P("mp", None),
        P(),
        P(None, None, "mp"),
        P(None, None, "mp"),
        P(None, "mp"),
        P(None, "mp"),
        P("nodes", None),
        P("nodes", None),
        P("nodes"),
        P("mp", None),
        P("mp", None),
        P(),
    )
    out_specs = (P("nodes", "mp"), P(("nodes", "mp"), None))
    return jax.shard_map(
        per_device, mesh=mesh, in_specs=in_specs, out_specs=out_specs, check_vma=False
    )
```

```python
import jax
import jax.numpy as jnp
from jax import lax
from jax.sharding import PartitionSpec as P

F32 = jnp.float32
BF16 = jnp.bfloat16


def one_hot(index, size, dtype=BF16):
    return (index[:, None] == lax.broadcasted_iota(jnp.int32, (1, size), 1)).astype(dtype)


def one_hot_t(index, size, dtype=BF16):
    return (lax.broadcasted_iota(jnp.int32, (size, 1), 0) == index[None, :]).astype(dtype)


def split_dot(x32, w):
    hi = x32.astype(BF16)
    lo = (x32 - hi.astype(F32)).astype(BF16)
    return jnp.dot(hi, w, preferred_element_type=F32) + jnp.dot(lo, w, preferred_element_type=F32)


def mp_reduce_scatter(x, axis, n, me):
    rows = x.shape[0] // n
    chunks = x.reshape(n, rows, x.shape[1])
    doubled = jnp.concatenate([chunks, chunks], axis=0)
    ahead = lax.dynamic_slice_in_dim(doubled, me, n, 0)
    total = ahead[0].astype(F32)
    for t in range(1, n):
        got = lax.ppermute(ahead[t], axis, [(i, (i + t) % n) for i in range(n)])
        total = total + got.astype(F32)
    return total


def mp_all_gather(piece, axis, n, me):
    rel = [piece]
    for t in range(1, n):
        rel.append(lax.ppermute(piece, axis, [(i, (i - t) % n) for i in range(n)]))
    rel = jnp.stack(rel + rel, axis=0)
    full = lax.dynamic_slice_in_dim(rel, (n - me) % n, n, 0)
    return full.reshape(n * piece.shape[0], piece.shape[1])


def per_device(
    event_feats,
    event_owner,
    event_slot,
    memory,
    w_msg_event,
    w_msg_state,
    b_msg,
    w_msg_out,
    b_out,
    w_input,
    w_hidden,
    b_input,
    b_hidden,
    state_slots,
    neighbours,
    query_slots,
    w_neigh,
    w_self,
    b_embed,
):
    owner_count = lax.axis_size("nodes")
    share_count = lax.axis_size("mp")
    mp_index = lax.axis_index("mp")
    event_rows = event_feats.shape[0]
    mem_rows = memory.shape[0]
    mem_width = memory.shape[1]
    col_share = mem_width // share_count
    capacity = 2 * event_rows // owner_count
    send_rows = owner_count * capacity

    owner = event_owner[:, 0]
    match = owner[:, None] == lax.broadcasted_iota(jnp.int32, (1, owner_count), 1)
    earlier = (
        lax.broadcasted_iota(jnp.int32, (event_rows, event_rows), 1)
        < lax.broadcasted_iota(jnp.int32, (event_rows, event_rows), 0)
    ).astype(BF16)
    before = jnp.dot(earlier, match.astype(BF16), preferred_element_type=F32)
    place = jnp.sum(jnp.where(match, before, 0.0), axis=1).astype(jnp.int32)
    per = capacity // share_count
    low = mp_index * per
    in_range = (place >= low) & (place < low + per)
    local = jnp.where(in_range, owner * per + (place - low), -1)
    route = one_hot_t(local, owner_count * per)
    feat_part = jnp.dot(route, event_feats, preferred_element_type=F32).astype(BF16)
    slot_col = jnp.broadcast_to((event_slot + 1).astype(BF16)[:, None], (event_rows, 128))
    id_part = jnp.dot(route, slot_col, preferred_element_type=F32)[:, 0] - 1.0
    feat_width = event_feats.shape[1]
    id_block = jnp.pad(id_part.reshape(owner_count, per), ((0, 0), (0, 128 - per)))
    payload = jnp.concatenate(
        [feat_part.reshape(owner_count, per * feat_width), id_block.astype(BF16)], axis=1
    )
    landed = lax.all_to_all(payload, "nodes", split_axis=0, concat_axis=0, tiled=True)
    pieces = [landed]
    for t in range(1, share_count):
        pieces.append(
            lax.ppermute(landed, "mp", [(i, (i - t) % share_count) for i in range(share_count)])
        )
    arrived = jnp.concatenate(
        [p[:, : per * feat_width].reshape(owner_count * per, feat_width) for p in pieces], axis=0
    )
    arrived_ids = jnp.concatenate(
        [p[:, per * feat_width : per * feat_width + per].reshape(owner_count * per) for p in pieces],
        axis=0,
    ).astype(jnp.int32)

    seg = one_hot_t(arrived_ids, mem_rows)
    seg_t = one_hot(arrived_ids, mem_rows)
    counts = jnp.sum(seg.astype(F32), axis=1)

    state_proj = jnp.dot(memory, w_msg_state, preferred_element_type=F32)
    sp_hi = state_proj.astype(BF16)
    sp_lo = (state_proj - sp_hi.astype(F32)).astype(BF16)
    gathered = jnp.dot(seg_t, sp_hi, preferred_element_type=F32) + jnp.dot(
        seg_t, sp_lo, preferred_element_type=F32
    )
    pre = jnp.dot(arrived, w_msg_event, preferred_element_type=F32) + gathered + b_msg
    hidden_msg = jax.nn.relu(pre).astype(BF16)
    hidden_sum = jnp.dot(seg, hidden_msg, preferred_element_type=F32)
    partial_total = split_dot(hidden_sum, w_msg_out)

    divisor = jnp.maximum(counts, 1.0)[:, None]
    reduced = mp_reduce_scatter(partial_total.astype(BF16), "mp", share_count, mp_index)
    msg_total = mp_all_gather(reduced.astype(BF16), "mp", share_count, mp_index).astype(F32)
    aggregate = (msg_total / divisor + b_out).astype(BF16)
    gates_in = (
        jnp.einsum("nd,gdc->gnc", aggregate, w_input, preferred_element_type=F32)
        + b_input[:, None, :]
    )
    gates_st = (
        jnp.einsum("nd,gdc->gnc", memory, w_hidden, preferred_element_type=F32)
        + b_hidden[:, None, :]
    )
    reset_gate = jax.nn.sigmoid(gates_in[0] + gates_st[0])
    update_gate = jax.nn.sigmoid(gates_in[1] + gates_st[1])
    candidate = jnp.tanh(gates_in[2] + reset_gate * gates_st[2])
    old_state = lax.dynamic_slice_in_dim(memory, mp_index * col_share, col_share, 1).astype(F32)
    updated = (1.0 - update_gate) * candidate + update_gate * old_state
    new_memory = jnp.where((counts > 0.0)[:, None], updated, old_state).astype(BF16)

    pick = one_hot(state_slots.reshape(-1), mem_rows)
    outgoing = jnp.dot(pick, new_memory, preferred_element_type=F32).astype(BF16)
    outgoing = outgoing.reshape(state_slots.shape[0], state_slots.shape[1], col_share)
    relayed = lax.all_to_all(outgoing, "nodes", split_axis=0, concat_axis=0, tiled=True)
    relayed = relayed.reshape(relayed.shape[0] * relayed.shape[1], col_share)
    recv_rows = relayed.shape[0]
    neigh_count = one_hot(neighbours[:, 0], recv_rows, F32)
    for k in range(1, neighbours.shape[1]):
        neigh_count = neigh_count + one_hot(neighbours[:, k], recv_rows, F32)
    neigh_total = jnp.dot(neigh_count.astype(BF16), relayed, preferred_element_type=F32)
    neigh_mean = (neigh_total / neighbours.shape[1]).astype(BF16)
    self_state = jnp.dot(
        one_hot(query_slots, mem_rows), new_memory, preferred_element_type=F32
    ).astype(BF16)
    summed = mp_reduce_scatter(
        (
            jnp.dot(neigh_mean, w_neigh, preferred_element_type=F32)
            + jnp.dot(self_state, w_self, preferred_element_type=F32)
        ).astype(BF16),
        "mp",
        share_count,
        mp_index,
    )
    embedding = jax.nn.relu(summed + b_embed).astype(BF16)
    return (new_memory, embedding)


def solution(mesh):
    in_specs = (
        P("nodes", None),
        P("nodes", None),
        P("nodes"),
        P("nodes", None),
        P(None, "mp"),
        P(None, "mp"),
        P("mp"),
        P("mp", None),
        P(),
        P(None, None, "mp"),
        P(None, None, "mp"),
        P(None, "mp"),
        P(None, "mp"),
        P("nodes", None),
        P("nodes", None),
        P("nodes"),
        P("mp", None),
        P("mp", None),
        P(),
    )
    out_specs = (P("nodes", "mp"), P(("nodes", "mp"), None))
    return jax.shard_map(
        per_device, mesh=mesh, in_specs=in_specs, out_specs=out_specs, check_vma=False
    )
```

```python
import jax
import jax.numpy as jnp
from jax import lax
from jax.sharding import PartitionSpec as P

F32 = jnp.float32
BF16 = jnp.bfloat16


def one_hot(index, size, dtype=BF16):
    return (index[:, None] == lax.broadcasted_iota(jnp.int32, (1, size), 1)).astype(dtype)


def one_hot_t(index, size, dtype=BF16):
    return (lax.broadcasted_iota(jnp.int32, (size, 1), 0) == index[None, :]).astype(dtype)


def split_dot(x32, w):
    hi = x32.astype(BF16)
    lo = (x32 - hi.astype(F32)).astype(BF16)
    return jnp.dot(hi, w, preferred_element_type=F32) + jnp.dot(lo, w, preferred_element_type=F32)


def mp_reduce_scatter(x, axis, n, me):
    rows = x.shape[0] // n
    chunks = x.reshape(n, rows, x.shape[1])
    doubled = jnp.concatenate([chunks, chunks], axis=0)
    ahead = lax.dynamic_slice_in_dim(doubled, me, n, 0)
    total = ahead[0].astype(F32)
    for t in range(1, n):
        got = lax.ppermute(ahead[t], axis, [(i, (i + t) % n) for i in range(n)])
        total = total + got.astype(F32)
    return total


def mp_all_gather(piece, axis, n, me):
    rel = [piece]
    for t in range(1, n):
        rel.append(lax.ppermute(piece, axis, [(i, (i - t) % n) for i in range(n)]))
    rel = jnp.stack(rel + rel, axis=0)
    full = lax.dynamic_slice_in_dim(rel, (n - me) % n, n, 0)
    return full.reshape(n * piece.shape[0], piece.shape[1])


def per_device(
    event_feats,
    event_owner,
    event_slot,
    memory,
    w_msg_event,
    w_msg_state,
    b_msg,
    w_msg_out,
    b_out,
    w_input,
    w_hidden,
    b_input,
    b_hidden,
    state_slots,
    neighbours,
    query_slots,
    w_neigh,
    w_self,
    b_embed,
):
    owner_count = lax.axis_size("nodes")
    share_count = lax.axis_size("mp")
    mp_index = lax.axis_index("mp")
    event_rows = event_feats.shape[0]
    mem_rows = memory.shape[0]
    mem_width = memory.shape[1]
    col_share = mem_width // share_count
    capacity = 2 * event_rows // owner_count
    send_rows = owner_count * capacity

    owner = event_owner[:, 0]
    match = owner[:, None] == lax.broadcasted_iota(jnp.int32, (1, owner_count), 1)
    earlier = (
        lax.broadcasted_iota(jnp.int32, (event_rows, event_rows), 1)
        < lax.broadcasted_iota(jnp.int32, (event_rows, event_rows), 0)
    ).astype(BF16)
    before = jnp.dot(earlier, match.astype(BF16), preferred_element_type=F32)
    place = jnp.sum(jnp.where(match, before, 0.0), axis=1).astype(jnp.int32)
    per = capacity // share_count
    low = mp_index * per
    in_range = (place >= low) & (place < low + per)
    local = jnp.where(in_range, (place - low) * owner_count + owner, -1)
    route = one_hot_t(local, per * owner_count)
    feat_width = event_feats.shape[1]
    feat_part = jnp.dot(route, event_feats, preferred_element_type=F32).astype(BF16)
    slot_col = jnp.broadcast_to((event_slot + 1).astype(BF16)[:, None], (event_rows, 128))
    id_part = jnp.dot(route, slot_col, preferred_element_type=F32)[:, 0] - 1.0
    id_plane = jnp.pad(id_part.reshape(per, owner_count).T, ((0, 0), (0, feat_width - per)))
    payload = jnp.concatenate(
        [feat_part.reshape(per, owner_count, feat_width), id_plane.astype(BF16)[None]], axis=0
    )
    landed = lax.all_to_all(payload, "nodes", split_axis=1, concat_axis=1, tiled=True)
    pieces = [landed]
    for t in range(1, share_count):
        pieces.append(
            lax.ppermute(landed, "mp", [(i, (i - t) % share_count) for i in range(share_count)])
        )
    arrived = jnp.concatenate(
        [p[:per].reshape(per * owner_count, feat_width) for p in pieces], axis=0
    )
    arrived_ids = jnp.concatenate(
        [p[per, :, :per].T.reshape(per * owner_count) for p in pieces], axis=0
    ).astype(jnp.int32)

    seg = one_hot_t(arrived_ids, mem_rows)
    seg_t = one_hot(arrived_ids, mem_rows)
    counts = jnp.sum(seg.astype(F32), axis=1)

    recv_rows = state_slots.shape[0] * state_slots.shape[1]
    neigh_count = one_hot(neighbours[:, 0], recv_rows, F32)
    for k in range(1, neighbours.shape[1]):
        neigh_count = neigh_count + one_hot(neighbours[:, k], recv_rows, F32)
    neigh_count = lax.optimization_barrier(neigh_count.astype(BF16))
    state_proj = jnp.dot(memory, w_msg_state, preferred_element_type=F32)
    sp_hi = state_proj.astype(BF16)
    sp_lo = (state_proj - sp_hi.astype(F32)).astype(BF16)
    lhs = jnp.concatenate([arrived, seg_t, seg_t], axis=1)
    rhs = jnp.concatenate([w_msg_event, sp_hi, sp_lo], axis=0)
    pre = jnp.dot(lhs, rhs, preferred_element_type=F32) + b_msg
    hidden_msg = jax.nn.relu(pre).astype(BF16)
    hidden_sum = jnp.dot(seg, hidden_msg, preferred_element_type=F32)
    partial_total = split_dot(hidden_sum, w_msg_out)

    divisor = jnp.maximum(counts, 1.0)[:, None]
    reduced = mp_reduce_scatter(partial_total.astype(BF16), "mp", share_count, mp_index)
    msg_total = mp_all_gather(reduced.astype(BF16), "mp", share_count, mp_index).astype(F32)
    aggregate = (msg_total / divisor + b_out).astype(BF16)
    gates_in = (
        jnp.einsum("nd,gdc->gnc", aggregate, w_input, preferred_element_type=F32)
        + b_input[:, None, :]
    )
    gates_st = (
        jnp.einsum("nd,gdc->gnc", memory, w_hidden, preferred_element_type=F32)
        + b_hidden[:, None, :]
    )
    reset_gate = jax.nn.sigmoid(gates_in[0] + gates_st[0])
    update_gate = jax.nn.sigmoid(gates_in[1] + gates_st[1])
    candidate = jnp.tanh(gates_in[2] + reset_gate * gates_st[2])
    old_state = lax.dynamic_slice_in_dim(memory, mp_index * col_share, col_share, 1).astype(F32)
    updated = (1.0 - update_gate) * candidate + update_gate * old_state
    new_memory = jnp.where((counts > 0.0)[:, None], updated, old_state).astype(BF16)

    pick = one_hot(state_slots.reshape(-1), mem_rows)
    outgoing = jnp.dot(pick, new_memory, preferred_element_type=F32).astype(BF16)
    outgoing = outgoing.reshape(state_slots.shape[0], state_slots.shape[1], col_share)
    relayed = lax.all_to_all(outgoing, "nodes", split_axis=0, concat_axis=0, tiled=True)
    relayed = relayed.reshape(relayed.shape[0] * relayed.shape[1], col_share)
    neigh_total = jnp.dot(neigh_count, relayed, preferred_element_type=F32)
    neigh_mean = (neigh_total / neighbours.shape[1]).astype(BF16)
    self_state = jnp.dot(
        one_hot(query_slots, mem_rows), new_memory, preferred_element_type=F32
    ).astype(BF16)
    summed = mp_reduce_scatter(
        (
            jnp.dot(neigh_mean, w_neigh, preferred_element_type=F32)
            + jnp.dot(self_state, w_self, preferred_element_type=F32)
        ).astype(BF16),
        "mp",
        share_count,
        mp_index,
    )
    embedding = jax.nn.relu(summed + b_embed).astype(BF16)
    return (new_memory, embedding)


def solution(mesh):
    in_specs = (
        P("nodes", None),
        P("nodes", None),
        P("nodes"),
        P("nodes", None),
        P(None, "mp"),
        P(None, "mp"),
        P("mp"),
        P("mp", None),
        P(),
        P(None, None, "mp"),
        P(None, None, "mp"),
        P(None, "mp"),
        P(None, "mp"),
        P("nodes", None),
        P("nodes", None),
        P("nodes"),
        P("mp", None),
        P("mp", None),
        P(),
    )
    out_specs = (P("nodes", "mp"), P(("nodes", "mp"), None))
    return jax.shard_map(
        per_device, mesh=mesh, in_specs=in_specs, out_specs=out_specs, check_vma=False
    )
```

```python
import jax
import jax.numpy as jnp
from jax import lax
from jax.sharding import PartitionSpec as P

F32 = jnp.float32
BF16 = jnp.bfloat16


def one_hot(index, size, dtype=BF16):
    return (index[:, None] == lax.broadcasted_iota(jnp.int32, (1, size), 1)).astype(dtype)


def one_hot_t(index, size, dtype=BF16):
    return (lax.broadcasted_iota(jnp.int32, (size, 1), 0) == index[None, :]).astype(dtype)


def split_dot(x32, w):
    hi = x32.astype(BF16)
    lo = (x32 - hi.astype(F32)).astype(BF16)
    return jnp.dot(hi, w, preferred_element_type=F32) + jnp.dot(lo, w, preferred_element_type=F32)


def mp_reduce_scatter(x, axis, n, me):
    rows = x.shape[0] // n
    chunks = x.reshape(n, rows, x.shape[1])
    doubled = jnp.concatenate([chunks, chunks], axis=0)
    ahead = lax.dynamic_slice_in_dim(doubled, me, n, 0)
    total = ahead[0].astype(F32)
    for t in range(1, n):
        got = lax.ppermute(ahead[t], axis, [(i, (i + t) % n) for i in range(n)])
        total = total + got.astype(F32)
    return total


def mp_all_gather(piece, axis, n, me):
    rel = [piece]
    for t in range(1, n):
        rel.append(lax.ppermute(piece, axis, [(i, (i - t) % n) for i in range(n)]))
    rel = jnp.stack(rel + rel, axis=0)
    full = lax.dynamic_slice_in_dim(rel, (n - me) % n, n, 0)
    return full.reshape(n * piece.shape[0], piece.shape[1])


def per_device(
    event_feats,
    event_owner,
    event_slot,
    memory,
    w_msg_event,
    w_msg_state,
    b_msg,
    w_msg_out,
    b_out,
    w_input,
    w_hidden,
    b_input,
    b_hidden,
    state_slots,
    neighbours,
    query_slots,
    w_neigh,
    w_self,
    b_embed,
):
    owner_count = lax.axis_size("nodes")
    share_count = lax.axis_size("mp")
    mp_index = lax.axis_index("mp")
    event_rows = event_feats.shape[0]
    mem_rows = memory.shape[0]
    mem_width = memory.shape[1]
    col_share = mem_width // share_count
    capacity = 2 * event_rows // owner_count
    send_rows = owner_count * capacity

    owner = event_owner[:, 0]
    match = owner[:, None] == lax.broadcasted_iota(jnp.int32, (1, owner_count), 1)
    earlier = (
        lax.broadcasted_iota(jnp.int32, (event_rows, event_rows), 1)
        < lax.broadcasted_iota(jnp.int32, (event_rows, event_rows), 0)
    ).astype(BF16)
    before = jnp.dot(earlier, match.astype(BF16), preferred_element_type=F32)
    place = jnp.sum(jnp.where(match, before, 0.0), axis=1).astype(jnp.int32)
    per = capacity // share_count
    low = mp_index * per
    in_range = (place >= low) & (place < low + per)
    local = jnp.where(in_range, owner * per + (place - low), -1)
    route = one_hot_t(local, owner_count * per)
    feat_width = event_feats.shape[1]
    feat_part = jnp.dot(route, event_feats, preferred_element_type=F32).astype(BF16)
    slot_col = jnp.broadcast_to((event_slot + 1).astype(BF16)[:, None], (event_rows, 128))
    id_part = jnp.dot(route, slot_col, preferred_element_type=F32)[:, 0] - 1.0
    id_block = jnp.pad(id_part.reshape(owner_count, per), ((0, 0), (0, 128 - per)))
    payload = jnp.concatenate(
        [feat_part.reshape(owner_count, per * feat_width), id_block.astype(BF16)], axis=1
    )
    landed = lax.all_to_all(payload, "nodes", split_axis=0, concat_axis=0, tiled=True)
    piece_rows = owner_count * per
    id_row = landed[:, per * feat_width : per * feat_width + per].reshape(1, piece_rows)
    id_rows = jnp.pad(id_row, ((0, 15), (0, feat_width - piece_rows)))
    mine = jnp.concatenate(
        [landed[:, : per * feat_width].reshape(piece_rows, feat_width), id_rows], axis=0
    )
    pieces = [mine]
    for t in range(1, share_count):
        pieces.append(
            lax.ppermute(mine, "mp", [(i, (i - t) % share_count) for i in range(share_count)])
        )

    recv_rows = state_slots.shape[0] * state_slots.shape[1]
    neigh_count = one_hot(neighbours[:, 0], recv_rows, F32)
    for k in range(1, neighbours.shape[1]):
        neigh_count = neigh_count + one_hot(neighbours[:, k], recv_rows, F32)
    neigh_count = lax.optimization_barrier(neigh_count.astype(BF16))
    state_proj = jnp.dot(memory, w_msg_state, preferred_element_type=F32)
    sp_hi = state_proj.astype(BF16)
    sp_lo = (state_proj - sp_hi.astype(F32)).astype(BF16)
    rhs = jnp.concatenate([w_msg_event, sp_hi, sp_lo], axis=0)

    hidden_sum = None
    counts = None
    for p in pieces:
        ids_p = p[piece_rows, :piece_rows].astype(jnp.int32)
        seg_t = one_hot(ids_p, mem_rows)
        seg = one_hot_t(ids_p, mem_rows)
        lhs = jnp.concatenate([p[:piece_rows], seg_t, seg_t], axis=1)
        pre = jnp.dot(lhs, rhs, preferred_element_type=F32) + b_msg
        hidden_msg = jax.nn.relu(pre).astype(BF16)
        part = jnp.dot(seg, hidden_msg, preferred_element_type=F32)
        cnt = jnp.sum(seg.astype(F32), axis=1)
        hidden_sum = part if hidden_sum is None else hidden_sum + part
        counts = cnt if counts is None else counts + cnt
    partial_total = split_dot(hidden_sum, w_msg_out)

    divisor = jnp.maximum(counts, 1.0)[:, None]
    reduced = mp_reduce_scatter(partial_total.astype(BF16), "mp", share_count, mp_index)
    msg_total = mp_all_gather(reduced.astype(BF16), "mp", share_count, mp_index).astype(F32)
    aggregate = (msg_total / divisor + b_out).astype(BF16)
    gates_in = (
        jnp.einsum("nd,gdc->gnc", aggregate, w_input, preferred_element_type=F32)
        + b_input[:, None, :]
    )
    gates_st = (
        jnp.einsum("nd,gdc->gnc", memory, w_hidden, preferred_element_type=F32)
        + b_hidden[:, None, :]
    )
    reset_gate = jax.nn.sigmoid(gates_in[0] + gates_st[0])
    update_gate = jax.nn.sigmoid(gates_in[1] + gates_st[1])
    candidate = jnp.tanh(gates_in[2] + reset_gate * gates_st[2])
    old_state = lax.dynamic_slice_in_dim(memory, mp_index * col_share, col_share, 1).astype(F32)
    updated = (1.0 - update_gate) * candidate + update_gate * old_state
    new_memory = jnp.where((counts > 0.0)[:, None], updated, old_state).astype(BF16)

    pick = one_hot(state_slots.reshape(-1), mem_rows)
    outgoing = jnp.dot(pick, new_memory, preferred_element_type=F32).astype(BF16)
    outgoing = outgoing.reshape(state_slots.shape[0], state_slots.shape[1], col_share)
    relayed = lax.all_to_all(outgoing, "nodes", split_axis=0, concat_axis=0, tiled=True)
    relayed = relayed.reshape(relayed.shape[0] * relayed.shape[1], col_share)
    neigh_total = jnp.dot(neigh_count, relayed, preferred_element_type=F32)
    neigh_mean = (neigh_total / neighbours.shape[1]).astype(BF16)
    self_state = jnp.dot(
        one_hot(query_slots, mem_rows), new_memory, preferred_element_type=F32
    ).astype(BF16)
    summed = mp_reduce_scatter(
        (
            jnp.dot(neigh_mean, w_neigh, preferred_element_type=F32)
            + jnp.dot(self_state, w_self, preferred_element_type=F32)
        ).astype(BF16),
        "mp",
        share_count,
        mp_index,
    )
    embedding = jax.nn.relu(summed + b_embed).astype(BF16)
    return (new_memory, embedding)


def solution(mesh):
    in_specs = (
        P("nodes", None),
        P("nodes", None),
        P("nodes"),
        P("nodes", None),
        P(None, "mp"),
        P(None, "mp"),
        P("mp"),
        P("mp", None),
        P(),
        P(None, None, "mp"),
        P(None, None, "mp"),
        P(None, "mp"),
        P(None, "mp"),
        P("nodes", None),
        P("nodes", None),
        P("nodes"),
        P("mp", None),
        P("mp", None),
        P(),
    )
    out_specs = (P("nodes", "mp"), P(("nodes", "mp"), None))
    return jax.shard_map(
        per_device, mesh=mesh, in_specs=in_specs, out_specs=out_specs, check_vma=False
    )
```

```python
import jax
import jax.numpy as jnp
from jax import lax
from jax.sharding import PartitionSpec as P

F32 = jnp.float32
BF16 = jnp.bfloat16


def one_hot(index, size, dtype=BF16):
    return (index[:, None] == lax.broadcasted_iota(jnp.int32, (1, size), 1)).astype(dtype)


def one_hot_t(index, size, dtype=BF16):
    return (lax.broadcasted_iota(jnp.int32, (size, 1), 0) == index[None, :]).astype(dtype)


def split_dot(x32, w):
    hi = x32.astype(BF16)
    lo = (x32 - hi.astype(F32)).astype(BF16)
    return jnp.dot(hi, w, preferred_element_type=F32) + jnp.dot(lo, w, preferred_element_type=F32)


def mp_reduce_scatter(x, axis, n, me):
    rows = x.shape[0] // n
    chunks = x.reshape(n, rows, x.shape[1])
    doubled = jnp.concatenate([chunks, chunks], axis=0)
    ahead = lax.dynamic_slice_in_dim(doubled, me, n, 0)
    total = ahead[0].astype(F32)
    for t in range(1, n):
        got = lax.ppermute(ahead[t], axis, [(i, (i + t) % n) for i in range(n)])
        total = total + got.astype(F32)
    return total


def mp_all_gather(piece, axis, n, me):
    rel = [piece]
    for t in range(1, n):
        rel.append(lax.ppermute(piece, axis, [(i, (i - t) % n) for i in range(n)]))
    rel = jnp.stack(rel + rel, axis=0)
    full = lax.dynamic_slice_in_dim(rel, (n - me) % n, n, 0)
    return full.reshape(n * piece.shape[0], piece.shape[1])


def per_device(
    event_feats,
    event_owner,
    event_slot,
    memory,
    w_msg_event,
    w_msg_state,
    b_msg,
    w_msg_out,
    b_out,
    w_input,
    w_hidden,
    b_input,
    b_hidden,
    state_slots,
    neighbours,
    query_slots,
    w_neigh,
    w_self,
    b_embed,
):
    owner_count = lax.axis_size("nodes")
    share_count = lax.axis_size("mp")
    mp_index = lax.axis_index("mp")
    event_rows = event_feats.shape[0]
    mem_rows = memory.shape[0]
    mem_width = memory.shape[1]
    col_share = mem_width // share_count
    capacity = 2 * event_rows // owner_count
    send_rows = owner_count * capacity

    owner = event_owner[:, 0]
    match = owner[:, None] == lax.broadcasted_iota(jnp.int32, (1, owner_count), 1)
    earlier = (
        lax.broadcasted_iota(jnp.int32, (event_rows, event_rows), 1)
        < lax.broadcasted_iota(jnp.int32, (event_rows, event_rows), 0)
    ).astype(BF16)
    before = jnp.dot(earlier, match.astype(BF16), preferred_element_type=F32)
    place = jnp.sum(jnp.where(match, before, 0.0), axis=1).astype(jnp.int32)
    per = capacity // share_count
    low = mp_index * per
    in_range = (place >= low) & (place < low + per)
    local = jnp.where(in_range, owner * per + (place - low), -1)
    route = one_hot_t(local, owner_count * per)
    feat_width = event_feats.shape[1]
    feat_part = jnp.dot(route, event_feats, preferred_element_type=F32).astype(BF16)
    slot_col = jnp.broadcast_to((event_slot + 1).astype(BF16)[:, None], (event_rows, 128))
    id_part = jnp.dot(route, slot_col, preferred_element_type=F32)[:, 0] - 1.0
    id_block = jnp.pad(id_part.reshape(owner_count, per), ((0, 0), (0, 128 - per)))
    payload = jnp.concatenate(
        [feat_part.reshape(owner_count, per * feat_width), id_block.astype(BF16)], axis=1
    )
    landed = lax.all_to_all(payload, "nodes", split_axis=0, concat_axis=0, tiled=True)
    piece_rows = owner_count * per
    id_row = landed[:, per * feat_width : per * feat_width + per].reshape(1, piece_rows)
    id_rows = jnp.pad(id_row, ((0, 15), (0, feat_width - piece_rows)))
    mine = jnp.concatenate(
        [landed[:, : per * feat_width].reshape(piece_rows, feat_width), id_rows], axis=0
    )
    if share_count == 4:
        up = [(i, (i + 1) % 4) for i in range(4)]
        down = [(i, (i - 1) % 4) for i in range(4)]
        from_below = lax.ppermute(mine, "mp", up)
        from_above = lax.ppermute(mine, "mp", down)
        cut = piece_rows // 2
        far_low = lax.ppermute(from_above[:cut], "mp", down)
        far_high = lax.ppermute(from_below[cut:], "mp", up)
        far = jnp.concatenate([far_low, far_high], axis=0)
        pieces = [mine, from_below, from_above, far]
    else:
        pieces = [mine]
        for t in range(1, share_count):
            pieces.append(
                lax.ppermute(mine, "mp", [(i, (i - t) % share_count) for i in range(share_count)])
            )

    recv_rows = state_slots.shape[0] * state_slots.shape[1]
    neigh_count = one_hot(neighbours[:, 0], recv_rows, F32)
    for k in range(1, neighbours.shape[1]):
        neigh_count = neigh_count + one_hot(neighbours[:, k], recv_rows, F32)
    neigh_count = lax.optimization_barrier(neigh_count.astype(BF16))
    state_proj = jnp.dot(memory, w_msg_state, preferred_element_type=F32)
    sp_hi = state_proj.astype(BF16)
    sp_lo = (state_proj - sp_hi.astype(F32)).astype(BF16)
    rhs = jnp.concatenate([w_msg_event, sp_hi, sp_lo], axis=0)

    hidden_sum = None
    counts = None
    for p in pieces:
        ids_p = p[piece_rows, :piece_rows].astype(jnp.int32)
        seg_t = one_hot(ids_p, mem_rows)
        seg = one_hot_t(ids_p, mem_rows)
        lhs = jnp.concatenate([p[:piece_rows], seg_t, seg_t], axis=1)
        pre = jnp.dot(lhs, rhs, preferred_element_type=F32) + b_msg
        hidden_msg = jax.nn.relu(pre).astype(BF16)
        part = jnp.dot(seg, hidden_msg, preferred_element_type=F32)
        cnt = jnp.sum(seg.astype(F32), axis=1)
        hidden_sum = part if hidden_sum is None else hidden_sum + part
        counts = cnt if counts is None else counts + cnt
    partial_total = split_dot(hidden_sum, w_msg_out)

    divisor = jnp.maximum(counts, 1.0)[:, None]
    reduced = mp_reduce_scatter(partial_total.astype(BF16), "mp", share_count, mp_index)
    msg_total = mp_all_gather(reduced.astype(BF16), "mp", share_count, mp_index).astype(F32)
    aggregate = (msg_total / divisor + b_out).astype(BF16)
    gates_in = (
        jnp.einsum("nd,gdc->gnc", aggregate, w_input, preferred_element_type=F32)
        + b_input[:, None, :]
    )
    gates_st = (
        jnp.einsum("nd,gdc->gnc", memory, w_hidden, preferred_element_type=F32)
        + b_hidden[:, None, :]
    )
    reset_gate = jax.nn.sigmoid(gates_in[0] + gates_st[0])
    update_gate = jax.nn.sigmoid(gates_in[1] + gates_st[1])
    candidate = jnp.tanh(gates_in[2] + reset_gate * gates_st[2])
    old_state = lax.dynamic_slice_in_dim(memory, mp_index * col_share, col_share, 1).astype(F32)
    updated = (1.0 - update_gate) * candidate + update_gate * old_state
    new_memory = jnp.where((counts > 0.0)[:, None], updated, old_state).astype(BF16)

    pick = one_hot(state_slots.reshape(-1), mem_rows)
    outgoing = jnp.dot(pick, new_memory, preferred_element_type=F32).astype(BF16)
    outgoing = outgoing.reshape(state_slots.shape[0], state_slots.shape[1], col_share)
    relayed = lax.all_to_all(outgoing, "nodes", split_axis=0, concat_axis=0, tiled=True)
    relayed = relayed.reshape(relayed.shape[0] * relayed.shape[1], col_share)
    neigh_total = jnp.dot(neigh_count, relayed, preferred_element_type=F32)
    neigh_mean = (neigh_total / neighbours.shape[1]).astype(BF16)
    self_state = jnp.dot(
        one_hot(query_slots, mem_rows), new_memory, preferred_element_type=F32
    ).astype(BF16)
    summed = mp_reduce_scatter(
        (
            jnp.dot(neigh_mean, w_neigh, preferred_element_type=F32)
            + jnp.dot(self_state, w_self, preferred_element_type=F32)
        ).astype(BF16),
        "mp",
        share_count,
        mp_index,
    )
    embedding = jax.nn.relu(summed + b_embed).astype(BF16)
    return (new_memory, embedding)


def solution(mesh):
    in_specs = (
        P("nodes", None),
        P("nodes", None),
        P("nodes"),
        P("nodes", None),
        P(None, "mp"),
        P(None, "mp"),
        P("mp"),
        P("mp", None),
        P(),
        P(None, None, "mp"),
        P(None, None, "mp"),
        P(None, "mp"),
        P(None, "mp"),
        P("nodes", None),
        P("nodes", None),
        P("nodes"),
        P("mp", None),
        P("mp", None),
        P(),
    )
    out_specs = (P("nodes", "mp"), P(("nodes", "mp"), None))
    return jax.shard_map(
        per_device, mesh=mesh, in_specs=in_specs, out_specs=out_specs, check_vma=False
    )
```

```python
import jax
import jax.numpy as jnp
from jax import lax
from jax.sharding import PartitionSpec as P

F32 = jnp.float32
BF16 = jnp.bfloat16


def one_hot(index, size, dtype=BF16):
    return (index[:, None] == lax.broadcasted_iota(jnp.int32, (1, size), 1)).astype(dtype)


def one_hot_t(index, size, dtype=BF16):
    return (lax.broadcasted_iota(jnp.int32, (size, 1), 0) == index[None, :]).astype(dtype)


def split_dot(x32, w):
    hi = x32.astype(BF16)
    lo = (x32 - hi.astype(F32)).astype(BF16)
    return jnp.dot(hi, w, preferred_element_type=F32) + jnp.dot(lo, w, preferred_element_type=F32)


def mp_reduce_scatter(x, axis, n, me):
    rows = x.shape[0] // n
    chunks = x.reshape(n, rows, x.shape[1])
    doubled = jnp.concatenate([chunks, chunks], axis=0)
    ahead = lax.dynamic_slice_in_dim(doubled, me, n, 0)
    total = ahead[0].astype(F32)
    for t in range(1, n):
        got = lax.ppermute(ahead[t], axis, [(i, (i + t) % n) for i in range(n)])
        total = total + got.astype(F32)
    return total


def mp_all_gather(piece, axis, n, me):
    rel = [piece]
    for t in range(1, n):
        rel.append(lax.ppermute(piece, axis, [(i, (i - t) % n) for i in range(n)]))
    rel = jnp.stack(rel + rel, axis=0)
    full = lax.dynamic_slice_in_dim(rel, (n - me) % n, n, 0)
    return full.reshape(n * piece.shape[0], piece.shape[1])


def ring_moves(n):
    return [(i, (i + 1) % n) for i in range(n)], [(i, (i - 1) % n) for i in range(n)]


def mp_reduce_scatter4(x, axis, me):
    n = 4
    rows = x.shape[0] // n
    half = rows // 2
    chunks = x.reshape(n, rows, x.shape[1])
    ahead = lax.dynamic_slice_in_dim(jnp.concatenate([chunks, chunks], axis=0), me, n, 0)
    up, down = ring_moves(n)
    up_a = lax.ppermute(jnp.concatenate([ahead[1], ahead[2][:half]], axis=0), axis, up)
    down_a = lax.ppermute(jnp.concatenate([ahead[3], ahead[2][half:]], axis=0), axis, down)
    up_b = lax.ppermute(up_a[rows:], axis, up)
    down_b = lax.ppermute(down_a[rows:], axis, down)
    far = jnp.concatenate([up_b, down_b], axis=0)
    return (
        ahead[0].astype(F32)
        + up_a[:rows].astype(F32)
        + down_a[:rows].astype(F32)
        + far.astype(F32)
    )


def mp_all_gather4(piece, axis, me):
    n = 4
    half = piece.shape[0] // 2
    up, down = ring_moves(n)
    below = lax.ppermute(piece, axis, up)
    above = lax.ppermute(piece, axis, down)
    far = jnp.concatenate(
        [lax.ppermute(above[:half], axis, down), lax.ppermute(below[half:], axis, up)], axis=0
    )
    rel = [piece, above, far, below]
    rel = jnp.stack(rel + rel, axis=0)
    full = lax.dynamic_slice_in_dim(rel, (n - me) % n, n, 0)
    return full.reshape(n * piece.shape[0], piece.shape[1])


def per_device(
    event_feats,
    event_owner,
    event_slot,
    memory,
    w_msg_event,
    w_msg_state,
    b_msg,
    w_msg_out,
    b_out,
    w_input,
    w_hidden,
    b_input,
    b_hidden,
    state_slots,
    neighbours,
    query_slots,
    w_neigh,
    w_self,
    b_embed,
):
    owner_count = lax.axis_size("nodes")
    share_count = lax.axis_size("mp")
    mp_index = lax.axis_index("mp")
    event_rows = event_feats.shape[0]
    mem_rows = memory.shape[0]
    mem_width = memory.shape[1]
    col_share = mem_width // share_count
    capacity = 2 * event_rows // owner_count
    send_rows = owner_count * capacity

    owner = event_owner[:, 0]
    match = owner[:, None] == lax.broadcasted_iota(jnp.int32, (1, owner_count), 1)
    earlier = (
        lax.broadcasted_iota(jnp.int32, (event_rows, event_rows), 1)
        < lax.broadcasted_iota(jnp.int32, (event_rows, event_rows), 0)
    ).astype(BF16)
    before = jnp.dot(earlier, match.astype(BF16), preferred_element_type=F32)
    place = jnp.sum(jnp.where(match, before, 0.0), axis=1).astype(jnp.int32)
    per = capacity // share_count
    low = mp_index * per
    in_range = (place >= low) & (place < low + per)
    local = jnp.where(in_range, owner * per + (place - low), -1)
    route = one_hot_t(local, owner_count * per)
    feat_width = event_feats.shape[1]
    feat_part = jnp.dot(route, event_feats, preferred_element_type=F32).astype(BF16)
    slot_col = jnp.broadcast_to((event_slot + 1).astype(BF16)[:, None], (event_rows, 128))
    id_part = jnp.dot(route, slot_col, preferred_element_type=F32)[:, 0] - 1.0
    id_block = jnp.pad(id_part.reshape(owner_count, per), ((0, 0), (0, 128 - per)))
    payload = jnp.concatenate(
        [feat_part.reshape(owner_count, per * feat_width), id_block.astype(BF16)], axis=1
    )
    landed = lax.all_to_all(payload, "nodes", split_axis=0, concat_axis=0, tiled=True)
    piece_rows = owner_count * per
    id_row = landed[:, per * feat_width : per * feat_width + per].reshape(1, piece_rows)
    id_rows = jnp.pad(id_row, ((0, 15), (0, feat_width - piece_rows)))
    mine = jnp.concatenate(
        [landed[:, : per * feat_width].reshape(piece_rows, feat_width), id_rows], axis=0
    )
    if share_count == 4:
        up = [(i, (i + 1) % 4) for i in range(4)]
        down = [(i, (i - 1) % 4) for i in range(4)]
        from_below = lax.ppermute(mine, "mp", up)
        from_above = lax.ppermute(mine, "mp", down)
        cut = piece_rows // 2
        far_low = lax.ppermute(from_above[:cut], "mp", down)
        far_high = lax.ppermute(from_below[cut:], "mp", up)
        far = jnp.concatenate([far_low, far_high], axis=0)
        pieces = [mine, from_below, from_above, far]
    else:
        pieces = [mine]
        for t in range(1, share_count):
            pieces.append(
                lax.ppermute(mine, "mp", [(i, (i - t) % share_count) for i in range(share_count)])
            )

    recv_rows = state_slots.shape[0] * state_slots.shape[1]
    neigh_count = one_hot(neighbours[:, 0], recv_rows, F32)
    for k in range(1, neighbours.shape[1]):
        neigh_count = neigh_count + one_hot(neighbours[:, k], recv_rows, F32)
    neigh_count = lax.optimization_barrier(neigh_count.astype(BF16))
    state_proj = jnp.dot(memory, w_msg_state, preferred_element_type=F32)
    sp_hi = state_proj.astype(BF16)
    sp_lo = (state_proj - sp_hi.astype(F32)).astype(BF16)
    rhs = jnp.concatenate([w_msg_event, sp_hi, sp_lo], axis=0)

    hidden_sum = None
    counts = None
    for p in pieces:
        ids_p = p[piece_rows, :piece_rows].astype(jnp.int32)
        seg_t = one_hot(ids_p, mem_rows)
        seg = one_hot_t(ids_p, mem_rows)
        lhs = jnp.concatenate([p[:piece_rows], seg_t, seg_t], axis=1)
        pre = jnp.dot(lhs, rhs, preferred_element_type=F32) + b_msg
        hidden_msg = jax.nn.relu(pre).astype(BF16)
        part = jnp.dot(seg, hidden_msg, preferred_element_type=F32)
        cnt = jnp.sum(seg.astype(F32), axis=1)
        hidden_sum = part if hidden_sum is None else hidden_sum + part
        counts = cnt if counts is None else counts + cnt
    partial_total = split_dot(hidden_sum, w_msg_out)

    divisor = jnp.maximum(counts, 1.0)[:, None]
    if share_count == 4:
        reduced = mp_reduce_scatter4(partial_total.astype(BF16), "mp", mp_index)
        msg_total = mp_all_gather4(reduced.astype(BF16), "mp", mp_index).astype(F32)
    else:
        reduced = mp_reduce_scatter(partial_total.astype(BF16), "mp", share_count, mp_index)
        msg_total = mp_all_gather(reduced.astype(BF16), "mp", share_count, mp_index).astype(F32)
    aggregate = (msg_total / divisor + b_out).astype(BF16)
    gates_in = (
        jnp.einsum("nd,gdc->gnc", aggregate, w_input, preferred_element_type=F32)
        + b_input[:, None, :]
    )
    gates_st = (
        jnp.einsum("nd,gdc->gnc", memory, w_hidden, preferred_element_type=F32)
        + b_hidden[:, None, :]
    )
    reset_gate = jax.nn.sigmoid(gates_in[0] + gates_st[0])
    update_gate = jax.nn.sigmoid(gates_in[1] + gates_st[1])
    candidate = jnp.tanh(gates_in[2] + reset_gate * gates_st[2])
    old_state = lax.dynamic_slice_in_dim(memory, mp_index * col_share, col_share, 1).astype(F32)
    updated = (1.0 - update_gate) * candidate + update_gate * old_state
    new_memory = jnp.where((counts > 0.0)[:, None], updated, old_state).astype(BF16)

    pick = one_hot(state_slots.reshape(-1), mem_rows)
    outgoing = jnp.dot(pick, new_memory, preferred_element_type=F32).astype(BF16)
    outgoing = outgoing.reshape(state_slots.shape[0], state_slots.shape[1], col_share)
    relayed = lax.all_to_all(outgoing, "nodes", split_axis=0, concat_axis=0, tiled=True)
    relayed = relayed.reshape(relayed.shape[0] * relayed.shape[1], col_share)
    neigh_total = jnp.dot(neigh_count, relayed, preferred_element_type=F32)
    neigh_mean = (neigh_total / neighbours.shape[1]).astype(BF16)
    self_state = jnp.dot(
        one_hot(query_slots, mem_rows), new_memory, preferred_element_type=F32
    ).astype(BF16)
    embed_partial = (
        jnp.dot(neigh_mean, w_neigh, preferred_element_type=F32)
        + jnp.dot(self_state, w_self, preferred_element_type=F32)
    ).astype(BF16)
    if share_count == 4:
        summed = mp_reduce_scatter4(embed_partial, "mp", mp_index)
    else:
        summed = mp_reduce_scatter(embed_partial, "mp", share_count, mp_index)
    embedding = jax.nn.relu(summed + b_embed).astype(BF16)
    return (new_memory, embedding)


def solution(mesh):
    in_specs = (
        P("nodes", None),
        P("nodes", None),
        P("nodes"),
        P("nodes", None),
        P(None, "mp"),
        P(None, "mp"),
        P("mp"),
        P("mp", None),
        P(),
        P(None, None, "mp"),
        P(None, None, "mp"),
        P(None, "mp"),
        P(None, "mp"),
        P("nodes", None),
        P("nodes", None),
        P("nodes"),
        P("mp", None),
        P("mp", None),
        P(),
    )
    out_specs = (P("nodes", "mp"), P(("nodes", "mp"), None))
    return jax.shard_map(
        per_device, mesh=mesh, in_specs=in_specs, out_specs=out_specs, check_vma=False
    )
```

```python
import jax
import jax.numpy as jnp
from jax import lax
from jax.sharding import PartitionSpec as P

F32 = jnp.float32
BF16 = jnp.bfloat16


def one_hot(index, size, dtype=BF16):
    return (index[:, None] == lax.broadcasted_iota(jnp.int32, (1, size), 1)).astype(dtype)


def one_hot_t(index, size, dtype=BF16):
    return (lax.broadcasted_iota(jnp.int32, (size, 1), 0) == index[None, :]).astype(dtype)


def split_dot(x32, w):
    hi = x32.astype(BF16)
    lo = (x32 - hi.astype(F32)).astype(BF16)
    return jnp.dot(hi, w, preferred_element_type=F32) + jnp.dot(lo, w, preferred_element_type=F32)


def mp_reduce_scatter(x, axis, n, me):
    rows = x.shape[0] // n
    chunks = x.reshape(n, rows, x.shape[1])
    doubled = jnp.concatenate([chunks, chunks], axis=0)
    ahead = lax.dynamic_slice_in_dim(doubled, me, n, 0)
    total = ahead[0].astype(F32)
    for t in range(1, n):
        got = lax.ppermute(ahead[t], axis, [(i, (i + t) % n) for i in range(n)])
        total = total + got.astype(F32)
    return total


def mp_all_gather(piece, axis, n, me):
    rel = [piece]
    for t in range(1, n):
        rel.append(lax.ppermute(piece, axis, [(i, (i - t) % n) for i in range(n)]))
    rel = jnp.stack(rel + rel, axis=0)
    full = lax.dynamic_slice_in_dim(rel, (n - me) % n, n, 0)
    return full.reshape(n * piece.shape[0], piece.shape[1])


def per_device(
    event_feats,
    event_owner,
    event_slot,
    memory,
    w_msg_event,
    w_msg_state,
    b_msg,
    w_msg_out,
    b_out,
    w_input,
    w_hidden,
    b_input,
    b_hidden,
    state_slots,
    neighbours,
    query_slots,
    w_neigh,
    w_self,
    b_embed,
):
    owner_count = lax.axis_size("nodes")
    share_count = lax.axis_size("mp")
    mp_index = lax.axis_index("mp")
    event_rows = event_feats.shape[0]
    mem_rows = memory.shape[0]
    mem_width = memory.shape[1]
    col_share = mem_width // share_count
    capacity = 2 * event_rows // owner_count

    owner = event_owner[:, 0]
    match = owner[:, None] == lax.broadcasted_iota(jnp.int32, (1, owner_count), 1)
    earlier = (
        lax.broadcasted_iota(jnp.int32, (event_rows, event_rows), 1)
        < lax.broadcasted_iota(jnp.int32, (event_rows, event_rows), 0)
    ).astype(BF16)
    before = jnp.dot(earlier, match.astype(BF16), preferred_element_type=F32)
    place = jnp.sum(jnp.where(match, before, 0.0), axis=1).astype(jnp.int32)
    per = capacity // share_count
    low = mp_index * per
    in_range = (place >= low) & (place < low + per)
    local = jnp.where(in_range, owner * per + (place - low), -1)
    route = one_hot_t(local, owner_count * per)
    feat_width = event_feats.shape[1]
    feat_part = jnp.dot(route, event_feats, preferred_element_type=F32).astype(BF16)
    slot_col = jnp.broadcast_to((event_slot + 1).astype(BF16)[:, None], (event_rows, 128))
    id_part = jnp.dot(route, slot_col, preferred_element_type=F32)[:, 0] - 1.0
    id_block = jnp.pad(id_part.reshape(owner_count, per), ((0, 0), (0, 128 - per)))
    payload = jnp.concatenate(
        [feat_part.reshape(owner_count, per * feat_width), id_block.astype(BF16)], axis=1
    )
    landed = lax.all_to_all(payload, "nodes", split_axis=0, concat_axis=0, tiled=True)
    piece_rows = owner_count * per
    id_row = landed[:, per * feat_width : per * feat_width + per].reshape(1, piece_rows)
    id_rows = jnp.pad(id_row, ((0, 15), (0, feat_width - piece_rows)))
    mine = jnp.concatenate(
        [landed[:, : per * feat_width].reshape(piece_rows, feat_width), id_rows], axis=0
    )
    if share_count == 4:
        up = [(i, (i + 1) % 4) for i in range(4)]
        down = [(i, (i - 1) % 4) for i in range(4)]
        from_below = lax.ppermute(mine, "mp", up)
        from_above = lax.ppermute(mine, "mp", down)
        cut = piece_rows // 2
        far_low = lax.ppermute(from_above[:cut], "mp", down)
        far_high = lax.ppermute(from_below[cut:], "mp", up)
        far = jnp.concatenate([far_low, far_high], axis=0)
        pieces = [mine, from_below, from_above, far]
    else:
        pieces = [mine]
        for t in range(1, share_count):
            pieces.append(
                lax.ppermute(mine, "mp", [(i, (i - t) % share_count) for i in range(share_count)])
            )

    recv_rows = state_slots.shape[0] * state_slots.shape[1]
    neigh_count = one_hot(neighbours[:, 0], recv_rows, F32)
    for k in range(1, neighbours.shape[1]):
        neigh_count = neigh_count + one_hot(neighbours[:, k], recv_rows, F32)
    neigh_count = lax.optimization_barrier(neigh_count.astype(BF16))
    pick = lax.optimization_barrier(one_hot(state_slots.reshape(-1), mem_rows))
    state_proj = jnp.dot(memory, w_msg_state, preferred_element_type=F32)
    sp_hi = state_proj.astype(BF16)
    sp_lo = (state_proj - sp_hi.astype(F32)).astype(BF16)
    rhs = jnp.concatenate([w_msg_event, sp_hi, sp_lo], axis=0)

    hidden_sum = None
    counts = None
    for p in pieces:
        ids_p = p[piece_rows, :piece_rows].astype(jnp.int32)
        seg_t = one_hot(ids_p, mem_rows)
        seg = one_hot_t(ids_p, mem_rows)
        lhs = jnp.concatenate([p[:piece_rows], seg_t, seg_t], axis=1)
        pre = jnp.dot(lhs, rhs, preferred_element_type=F32) + b_msg
        hidden_msg = jax.nn.relu(pre).astype(BF16)
        part = jnp.dot(seg, hidden_msg, preferred_element_type=F32)
        cnt = jnp.sum(seg.astype(F32), axis=1)
        hidden_sum = part if hidden_sum is None else hidden_sum + part
        counts = cnt if counts is None else counts + cnt
    partial_total = split_dot(hidden_sum, w_msg_out)

    divisor = jnp.maximum(counts, 1.0)[:, None]
    reduced = mp_reduce_scatter(partial_total.astype(BF16), "mp", share_count, mp_index)
    msg_total = mp_all_gather(reduced.astype(BF16), "mp", share_count, mp_index).astype(F32)
    aggregate = (msg_total / divisor + b_out).astype(BF16)
    gates_in = (
        jnp.einsum("nd,gdc->gnc", aggregate, w_input, preferred_element_type=F32)
        + b_input[:, None, :]
    )
    gates_st = (
        jnp.einsum("nd,gdc->gnc", memory, w_hidden, preferred_element_type=F32)
        + b_hidden[:, None, :]
    )
    reset_gate = jax.nn.sigmoid(gates_in[0] + gates_st[0])
    update_gate = jax.nn.sigmoid(gates_in[1] + gates_st[1])
    candidate = jnp.tanh(gates_in[2] + reset_gate * gates_st[2])
    old_state = lax.dynamic_slice_in_dim(memory, mp_index * col_share, col_share, 1).astype(F32)
    updated = (1.0 - update_gate) * candidate + update_gate * old_state
    new_memory = jnp.where((counts > 0.0)[:, None], updated, old_state).astype(BF16)

    outgoing = jnp.dot(pick, new_memory, preferred_element_type=F32).astype(BF16)
    outgoing = outgoing.reshape(state_slots.shape[0], state_slots.shape[1], col_share)
    self_state = jnp.dot(
        one_hot(query_slots, mem_rows), new_memory, preferred_element_type=F32
    ).astype(BF16)
    self_part = lax.optimization_barrier(jnp.dot(self_state, w_self, preferred_element_type=F32))
    relayed = lax.all_to_all(outgoing, "nodes", split_axis=0, concat_axis=0, tiled=True)
    relayed = relayed.reshape(relayed.shape[0] * relayed.shape[1], col_share)
    neigh_total = jnp.dot(neigh_count, relayed, preferred_element_type=F32)
    neigh_mean = (neigh_total / neighbours.shape[1]).astype(BF16)
    summed = mp_reduce_scatter(
        (
            jnp.dot(neigh_mean, w_neigh, preferred_element_type=F32)
            + self_part
        ).astype(BF16),
        "mp",
        share_count,
        mp_index,
    )
    embedding = jax.nn.relu(summed + b_embed).astype(BF16)
    return (new_memory, embedding)


def solution(mesh):
    in_specs = (
        P("nodes", None),
        P("nodes", None),
        P("nodes"),
        P("nodes", None),
        P(None, "mp"),
        P(None, "mp"),
        P("mp"),
        P("mp", None),
        P(),
        P(None, None, "mp"),
        P(None, None, "mp"),
        P(None, "mp"),
        P(None, "mp"),
        P("nodes", None),
        P("nodes", None),
        P("nodes"),
        P("mp", None),
        P("mp", None),
        P(),
    )
    out_specs = (P("nodes", "mp"), P(("nodes", "mp"), None))

    return jax.shard_map(
        per_device, mesh=mesh, in_specs=in_specs, out_specs=out_specs, check_vma=False
    )
```

```python
import jax
import jax.numpy as jnp
from jax import lax
from jax.sharding import PartitionSpec as P

F32 = jnp.float32
BF16 = jnp.bfloat16


def one_hot(index, size, dtype=BF16):
    return (index[:, None] == lax.broadcasted_iota(jnp.int32, (1, size), 1)).astype(dtype)


def one_hot_t(index, size, dtype=BF16):
    return (lax.broadcasted_iota(jnp.int32, (size, 1), 0) == index[None, :]).astype(dtype)


def split_dot(x32, w):
    hi = x32.astype(BF16)
    lo = (x32 - hi.astype(F32)).astype(BF16)
    return jnp.dot(hi, w, preferred_element_type=F32) + jnp.dot(lo, w, preferred_element_type=F32)


def mp_reduce_scatter(x, axis, n, me):
    rows = x.shape[0] // n
    chunks = x.reshape(n, rows, x.shape[1])
    doubled = jnp.concatenate([chunks, chunks], axis=0)
    ahead = lax.dynamic_slice_in_dim(doubled, me, n, 0)
    total = ahead[0].astype(F32)
    for t in range(1, n):
        got = lax.ppermute(ahead[t], axis, [(i, (i + t) % n) for i in range(n)])
        total = total + got.astype(F32)
    return total


def mp_all_gather(piece, axis, n, me):
    rel = [piece]
    for t in range(1, n):
        rel.append(lax.ppermute(piece, axis, [(i, (i - t) % n) for i in range(n)]))
    rel = jnp.stack(rel + rel, axis=0)
    full = lax.dynamic_slice_in_dim(rel, (n - me) % n, n, 0)
    return full.reshape(n * piece.shape[0], piece.shape[1])


def per_device(
    event_feats,
    event_owner,
    event_slot,
    memory,
    w_msg_event,
    w_msg_state,
    b_msg,
    w_msg_out,
    b_out,
    w_input,
    w_hidden,
    b_input,
    b_hidden,
    state_slots,
    neighbours,
    query_slots,
    w_neigh,
    w_self,
    b_embed,
):
    owner_count = lax.axis_size("nodes")
    share_count = lax.axis_size("mp")
    mp_index = lax.axis_index("mp")
    event_rows = event_feats.shape[0]
    mem_rows = memory.shape[0]
    mem_width = memory.shape[1]
    col_share = mem_width // share_count
    capacity = 2 * event_rows // owner_count

    owner = event_owner[:, 0]
    match = owner[:, None] == lax.broadcasted_iota(jnp.int32, (1, owner_count), 1)
    earlier = (
        lax.broadcasted_iota(jnp.int32, (event_rows, event_rows), 1)
        < lax.broadcasted_iota(jnp.int32, (event_rows, event_rows), 0)
    ).astype(BF16)
    before = jnp.dot(earlier, match.astype(BF16), preferred_element_type=F32)
    place = jnp.sum(jnp.where(match, before, 0.0), axis=1).astype(jnp.int32)
    per = capacity // share_count
    low = mp_index * per
    in_range = (place >= low) & (place < low + per)
    local = jnp.where(in_range, owner * per + (place - low), -1)
    route = one_hot_t(local, owner_count * per)
    feat_width = event_feats.shape[1]
    feat_part = jnp.dot(route, event_feats, preferred_element_type=F32).astype(BF16)
    slot_col = jnp.broadcast_to((event_slot + 1).astype(BF16)[:, None], (event_rows, 128))
    id_part = jnp.dot(route, slot_col, preferred_element_type=F32)[:, 0] - 1.0
    id_block = jnp.pad(id_part.reshape(owner_count, per), ((0, 0), (0, 128 - per)))
    width = per * feat_width + 128
    payload = jnp.concatenate(
        [feat_part.reshape(owner_count, per * feat_width), id_block.astype(BF16)], axis=1
    ).reshape(owner_count, 2, width // 2)
    landed = lax.all_to_all(payload, "nodes", split_axis=0, concat_axis=0, tiled=True)
    landed = landed.reshape(owner_count, width)
    piece_rows = owner_count * per
    id_row = landed[:, per * feat_width : per * feat_width + per].reshape(1, piece_rows)
    id_rows = jnp.pad(id_row, ((0, 15), (0, feat_width - piece_rows)))
    mine = jnp.concatenate(
        [landed[:, : per * feat_width].reshape(piece_rows, feat_width), id_rows], axis=0
    )
    if share_count == 4:
        up = [(i, (i + 1) % 4) for i in range(4)]
        down = [(i, (i - 1) % 4) for i in range(4)]
        from_below = lax.ppermute(mine, "mp", up)
        from_above = lax.ppermute(mine, "mp", down)
        cut = piece_rows // 2
        far_low = lax.ppermute(from_above[:cut], "mp", down)
        far_high = lax.ppermute(from_below[cut:], "mp", up)
        far = jnp.concatenate([far_low, far_high], axis=0)
        pieces = [mine, from_below, from_above, far]
    else:
        pieces = [mine]
        for t in range(1, share_count):
            pieces.append(
                lax.ppermute(mine, "mp", [(i, (i - t) % share_count) for i in range(share_count)])
            )

    recv_rows = state_slots.shape[0] * state_slots.shape[1]
    neigh_count = one_hot(neighbours[:, 0], recv_rows, F32)
    for k in range(1, neighbours.shape[1]):
        neigh_count = neigh_count + one_hot(neighbours[:, k], recv_rows, F32)
    neigh_count = lax.optimization_barrier(neigh_count.astype(BF16))
    state_proj = jnp.dot(memory, w_msg_state, preferred_element_type=F32)
    sp_hi = state_proj.astype(BF16)
    sp_lo = (state_proj - sp_hi.astype(F32)).astype(BF16)
    rhs = jnp.concatenate([w_msg_event, sp_hi, sp_lo], axis=0)

    hidden_sum = None
    counts = None
    for p in pieces:
        ids_p = p[piece_rows, :piece_rows].astype(jnp.int32)
        seg_t = one_hot(ids_p, mem_rows)
        seg = one_hot_t(ids_p, mem_rows)
        lhs = jnp.concatenate([p[:piece_rows], seg_t, seg_t], axis=1)
        pre = jnp.dot(lhs, rhs, preferred_element_type=F32) + b_msg
        hidden_msg = jax.nn.relu(pre).astype(BF16)
        part = jnp.dot(seg, hidden_msg, preferred_element_type=F32)
        cnt = jnp.sum(seg.astype(F32), axis=1)
        hidden_sum = part if hidden_sum is None else hidden_sum + part
        counts = cnt if counts is None else counts + cnt
    partial_total = split_dot(hidden_sum, w_msg_out)

    divisor = jnp.maximum(counts, 1.0)[:, None]
    reduced = mp_reduce_scatter(partial_total.astype(BF16), "mp", share_count, mp_index)
    msg_total = mp_all_gather(reduced.astype(BF16), "mp", share_count, mp_index).astype(F32)
    aggregate = (msg_total / divisor + b_out).astype(BF16)
    gates_in = (
        jnp.einsum("nd,gdc->gnc", aggregate, w_input, preferred_element_type=F32)
        + b_input[:, None, :]
    )
    gates_st = (
        jnp.einsum("nd,gdc->gnc", memory, w_hidden, preferred_element_type=F32)
        + b_hidden[:, None, :]
    )
    reset_gate = jax.nn.sigmoid(gates_in[0] + gates_st[0])
    update_gate = jax.nn.sigmoid(gates_in[1] + gates_st[1])
    candidate = jnp.tanh(gates_in[2] + reset_gate * gates_st[2])
    old_state = lax.dynamic_slice_in_dim(memory, mp_index * col_share, col_share, 1).astype(F32)
    updated = (1.0 - update_gate) * candidate + update_gate * old_state
    new_memory = jnp.where((counts > 0.0)[:, None], updated, old_state).astype(BF16)

    pick = one_hot(state_slots.reshape(-1), mem_rows)
    outgoing = jnp.dot(pick, new_memory, preferred_element_type=F32).astype(BF16)
    outgoing = outgoing.reshape(state_slots.shape[0], state_slots.shape[1], col_share)
    self_state = jnp.dot(
        one_hot(query_slots, mem_rows), new_memory, preferred_element_type=F32
    ).astype(BF16)
    self_part = lax.optimization_barrier(jnp.dot(self_state, w_self, preferred_element_type=F32))
    relayed = lax.all_to_all(outgoing, "nodes", split_axis=0, concat_axis=0, tiled=True)
    relayed = relayed.reshape(relayed.shape[0] * relayed.shape[1], col_share)
    neigh_total = jnp.dot(neigh_count, relayed, preferred_element_type=F32)
    neigh_mean = (neigh_total / neighbours.shape[1]).astype(BF16)
    summed = mp_reduce_scatter(
        (
            jnp.dot(neigh_mean, w_neigh, preferred_element_type=F32)
            + self_part
        ).astype(BF16),
        "mp",
        share_count,
        mp_index,
    )
    embedding = jax.nn.relu(summed + b_embed).astype(BF16)
    return (new_memory, embedding)


def solution(mesh):
    in_specs = (
        P("nodes", None),
        P("nodes", None),
        P("nodes"),
        P("nodes", None),
        P(None, "mp"),
        P(None, "mp"),
        P("mp"),
        P("mp", None),
        P(),
        P(None, None, "mp"),
        P(None, None, "mp"),
        P(None, "mp"),
        P(None, "mp"),
        P("nodes", None),
        P("nodes", None),
        P("nodes"),
        P("mp", None),
        P("mp", None),
        P(),
    )
    out_specs = (P("nodes", "mp"), P(("nodes", "mp"), None))

    return jax.shard_map(
        per_device, mesh=mesh, in_specs=in_specs, out_specs=out_specs, check_vma=False
    )
```

```python
import jax
import jax.numpy as jnp
from jax import lax
from jax.sharding import PartitionSpec as P

F32 = jnp.float32
BF16 = jnp.bfloat16


def one_hot(index, size, dtype=BF16):
    return (index[:, None] == lax.broadcasted_iota(jnp.int32, (1, size), 1)).astype(dtype)


def one_hot_t(index, size, dtype=BF16):
    return (lax.broadcasted_iota(jnp.int32, (size, 1), 0) == index[None, :]).astype(dtype)


def split_dot(x32, w):
    hi = x32.astype(BF16)
    lo = (x32 - hi.astype(F32)).astype(BF16)
    return jnp.dot(hi, w, preferred_element_type=F32) + jnp.dot(lo, w, preferred_element_type=F32)


def mp_reduce_scatter(x, axis, n, me):
    rows = x.shape[0] // n
    chunks = x.reshape(n, rows, x.shape[1])
    doubled = jnp.concatenate([chunks, chunks], axis=0)
    ahead = lax.dynamic_slice_in_dim(doubled, me, n, 0)
    total = ahead[0].astype(F32)
    for t in range(1, n):
        got = lax.ppermute(ahead[t], axis, [(i, (i + t) % n) for i in range(n)])
        total = total + got.astype(F32)
    return total


def mp_all_gather(piece, axis, n, me):
    rel = [piece]
    for t in range(1, n):
        rel.append(lax.ppermute(piece, axis, [(i, (i - t) % n) for i in range(n)]))
    rel = jnp.stack(rel + rel, axis=0)
    full = lax.dynamic_slice_in_dim(rel, (n - me) % n, n, 0)
    return full.reshape(n * piece.shape[0], piece.shape[1])


def per_device(
    event_feats,
    event_owner,
    event_slot,
    memory,
    w_msg_event,
    w_msg_state,
    b_msg,
    w_msg_out,
    b_out,
    w_input,
    w_hidden,
    b_input,
    b_hidden,
    state_slots,
    neighbours,
    query_slots,
    w_neigh,
    w_self,
    b_embed,
):
    owner_count = lax.axis_size("nodes")
    share_count = lax.axis_size("mp")
    mp_index = lax.axis_index("mp")
    event_rows = event_feats.shape[0]
    mem_rows = memory.shape[0]
    mem_width = memory.shape[1]
    col_share = mem_width // share_count
    capacity = 2 * event_rows // owner_count

    owner = event_owner[:, 0]
    match = owner[:, None] == lax.broadcasted_iota(jnp.int32, (1, owner_count), 1)
    blk = 128
    nblk = event_rows // blk
    m_blk = match.astype(BF16).reshape(nblk, blk, owner_count)
    tri = (
        lax.broadcasted_iota(jnp.int32, (blk, blk), 1) < lax.broadcasted_iota(jnp.int32, (blk, blk), 0)
    ).astype(BF16)
    inblock = jnp.einsum("rs,bso->bro", tri, m_blk, preferred_element_type=F32)
    block_sum = jnp.sum(m_blk.astype(F32), axis=1)
    tri_b = (
        lax.broadcasted_iota(jnp.int32, (nblk, nblk), 1) < lax.broadcasted_iota(jnp.int32, (nblk, nblk), 0)
    ).astype(F32)
    offset = jnp.dot(tri_b, block_sum, precision=lax.Precision.HIGHEST)
    before = (inblock + offset[:, None, :]).reshape(event_rows, owner_count)
    place = jnp.sum(jnp.where(match, before, 0.0), axis=1).astype(jnp.int32)
    per = capacity // share_count
    low = mp_index * per
    in_range = (place >= low) & (place < low + per)
    local = jnp.where(in_range, owner * per + (place - low), -1)
    route = one_hot_t(local, owner_count * per)
    feat_width = event_feats.shape[1]
    feat_part = jnp.dot(route, event_feats, preferred_element_type=F32).astype(BF16)
    slot_col = jnp.broadcast_to((event_slot + 1).astype(BF16)[:, None], (event_rows, 128))
    id_part = jnp.dot(route, slot_col, preferred_element_type=F32)[:, 0] - 1.0
    id_block = jnp.pad(id_part.reshape(owner_count, per), ((0, 0), (0, 128 - per)))
    width = per * feat_width + 128
    payload = jnp.concatenate(
        [feat_part.reshape(owner_count, per * feat_width), id_block.astype(BF16)], axis=1
    ).reshape(owner_count, 2, width // 2)
    landed = lax.all_to_all(payload, "nodes", split_axis=0, concat_axis=0, tiled=True)
    landed = landed.reshape(owner_count, width)
    piece_rows = owner_count * per
    id_row = landed[:, per * feat_width : per * feat_width + per].reshape(1, piece_rows)
    id_rows = jnp.pad(id_row, ((0, 15), (0, feat_width - piece_rows)))
    mine = jnp.concatenate(
        [landed[:, : per * feat_width].reshape(piece_rows, feat_width), id_rows], axis=0
    )
    if share_count == 4:
        up = [(i, (i + 1) % 4) for i in range(4)]
        down = [(i, (i - 1) % 4) for i in range(4)]
        from_below = lax.ppermute(mine, "mp", up)
        from_above = lax.ppermute(mine, "mp", down)
        cut = piece_rows // 2
        far_low = lax.ppermute(from_above[:cut], "mp", down)
        far_high = lax.ppermute(from_below[cut:], "mp", up)
        far = jnp.concatenate([far_low, far_high], axis=0)
        pieces = [mine, from_below, from_above, far]
    else:
        pieces = [mine]
        for t in range(1, share_count):
            pieces.append(
                lax.ppermute(mine, "mp", [(i, (i - t) % share_count) for i in range(share_count)])
            )

    recv_rows = state_slots.shape[0] * state_slots.shape[1]
    neigh_count = one_hot(neighbours[:, 0], recv_rows, F32)
    for k in range(1, neighbours.shape[1]):
        neigh_count = neigh_count + one_hot(neighbours[:, k], recv_rows, F32)
    neigh_count = lax.optimization_barrier(neigh_count.astype(BF16))
    state_proj = jnp.dot(memory, w_msg_state, preferred_element_type=F32)
    sp_hi = state_proj.astype(BF16)
    sp_lo = (state_proj - sp_hi.astype(F32)).astype(BF16)
    rhs = jnp.concatenate([w_msg_event, sp_hi, sp_lo], axis=0)

    hidden_sum = None
    counts = None
    for p in pieces:
        ids_p = p[piece_rows, :piece_rows].astype(jnp.int32)
        seg_t = one_hot(ids_p, mem_rows)
        seg = one_hot_t(ids_p, mem_rows)
        lhs = jnp.concatenate([p[:piece_rows], seg_t, seg_t], axis=1)
        pre = jnp.dot(lhs, rhs, preferred_element_type=F32) + b_msg
        hidden_msg = jax.nn.relu(pre).astype(BF16)
        part = jnp.dot(seg, hidden_msg, preferred_element_type=F32)
        cnt = jnp.sum(seg.astype(F32), axis=1)
        hidden_sum = part if hidden_sum is None else hidden_sum + part
        counts = cnt if counts is None else counts + cnt
    partial_total = split_dot(hidden_sum, w_msg_out)

    divisor = jnp.maximum(counts, 1.0)[:, None]
    reduced = mp_reduce_scatter(partial_total.astype(BF16), "mp", share_count, mp_index)
    msg_total = mp_all_gather(reduced.astype(BF16), "mp", share_count, mp_index).astype(F32)
    aggregate = (msg_total / divisor + b_out).astype(BF16)
    gates_in = (
        jnp.einsum("nd,gdc->gnc", aggregate, w_input, preferred_element_type=F32)
        + b_input[:, None, :]
    )
    gates_st = (
        jnp.einsum("nd,gdc->gnc", memory, w_hidden, preferred_element_type=F32)
        + b_hidden[:, None, :]
    )
    reset_gate = jax.nn.sigmoid(gates_in[0] + gates_st[0])
    update_gate = jax.nn.sigmoid(gates_in[1] + gates_st[1])
    candidate = jnp.tanh(gates_in[2] + reset_gate * gates_st[2])
    old_state = lax.dynamic_slice_in_dim(memory, mp_index * col_share, col_share, 1).astype(F32)
    updated = (1.0 - update_gate) * candidate + update_gate * old_state
    new_memory = jnp.where((counts > 0.0)[:, None], updated, old_state).astype(BF16)

    pick = one_hot(state_slots.reshape(-1), mem_rows)
    outgoing = jnp.dot(pick, new_memory, preferred_element_type=F32).astype(BF16)
    outgoing = outgoing.reshape(state_slots.shape[0], state_slots.shape[1], col_share)
    self_state = jnp.dot(
        one_hot(query_slots, mem_rows), new_memory, preferred_element_type=F32
    ).astype(BF16)
    self_part = lax.optimization_barrier(jnp.dot(self_state, w_self, preferred_element_type=F32))
    relayed = lax.all_to_all(outgoing, "nodes", split_axis=0, concat_axis=0, tiled=True)
    relayed = relayed.reshape(relayed.shape[0] * relayed.shape[1], col_share)
    neigh_total = jnp.dot(neigh_count, relayed, preferred_element_type=F32)
    neigh_mean = (neigh_total / neighbours.shape[1]).astype(BF16)
    summed = mp_reduce_scatter(
        (
            jnp.dot(neigh_mean, w_neigh, preferred_element_type=F32)
            + self_part
        ).astype(BF16),
        "mp",
        share_count,
        mp_index,
    )
    embedding = jax.nn.relu(summed + b_embed).astype(BF16)
    return (new_memory, embedding)


def solution(mesh):
    in_specs = (
        P("nodes", None),
        P("nodes", None),
        P("nodes"),
        P("nodes", None),
        P(None, "mp"),
        P(None, "mp"),
        P("mp"),
        P("mp", None),
        P(),
        P(None, None, "mp"),
        P(None, None, "mp"),
        P(None, "mp"),
        P(None, "mp"),
        P("nodes", None),
        P("nodes", None),
        P("nodes"),
        P("mp", None),
        P("mp", None),
        P(),
    )
    out_specs = (P("nodes", "mp"), P(("nodes", "mp"), None))

    return jax.shard_map(
        per_device, mesh=mesh, in_specs=in_specs, out_specs=out_specs, check_vma=False
    )
```
